128 devices in a mesh: dp: 4 (over x_lo, core), ens: 32 (over x_hi, y, z).
Axes of the slice: x: 4 (x_hi: 2, x_lo: 2; x = x_hi * 2 + x_lo), y: 4, z: 4, core: 2. Of those that a mesh axis runs over, the one named last changes fastest.
Arguments:
- embed: bfloat16 [4, 512, 128, 256], P('dp', 'ens'), may hold values from -6 to 6
- counts: int32 [4, 512], P('dp', 'ens'), may hold values from 4 to 128, as said below
- member: int32 [4, 512], P('dp', 'ens'), may hold values from 0 to 3, as said below
- bins: int32 [4, 512, 128, 128], P('dp', 'ens'), may hold values from 0 to 7
- masses: float32 [4, 4], P('dp'), may hold values from -1.5 to 1.5
- gain_attn: float32 [1, 256], replicated, may hold values from 0.25 to 1.75
- w_qkv: bfloat16 [1, 256, 768], replicated, may hold values from -0.375 to 0.375
- w_out: bfloat16 [1, 256, 256], replicated, may hold values from -0.375 to 0.375
- pair_table: float32 [1, 8, 8], replicated, may hold values from -4 to 4
- gain_ffn: float32 [1, 256], replicated, may hold values from 0.25 to 1.75
- w_up: bfloat16 [1, 256, 1024], replicated, may hold values from -0.375 to 0.375
- w_down: bfloat16 [1, 1024, 256], replicated, may hold values from -0.1875 to 0.1875
- w_phi: bfloat16 [256, 256], replicated, may hold values from -0.375 to 0.375
- w_mean: float32 [256], replicated, may hold values from -0.375 to 0.375
- w_scale: float32 [256], replicated, may hold values from -0.375 to 0.375
Outputs:
- neg_loglik: float32 [4, 4], P('dp')
- grad_gain_attn: float32 [1, 256], replicated
- grad_w_qkv: float32 [1, 256, 768], replicated
- grad_w_out: float32 [1, 256, 256], replicated
- grad_pair_table: float32 [1, 8, 8], replicated
- grad_gain_ffn: float32 [1, 256], replicated
- grad_w_up: float32 [1, 256, 1024], replicated
- grad_w_down: float32 [1, 1024, 256], replicated
- grad_w_phi: float32 [256, 256], replicated
- grad_w_mean: float32 [256], replicated
- grad_w_scale: float32 [256], replicated
The draws below stay inside these ranges and needn't reach their ends.
Inputs may be any that keep to these rules, and one draw needn't show every extreme that they name: `counts`: every run of 16 consecutive jets of a group holds a jet with 128 constituents. `member`: every run of 16 consecutive jets of a group holds at least one jet of each ensemble.
All inputs are finite; a program needn't handle non-finite values.
Results may differ from the reference program's by a relative error of at most 0.028.
Values sent between devices are 32-bit elements; how exact they have to be, the bound alone decides.
No kernel may reach another device: no remote copies, remote signals or barrier semaphores. Data moves between devices by JAX's collectives and lax.ppermute only.
A program may use at most 128 MiB of HBM per device.

```python
import math
import jax
import jax.numpy as jnp
from jax import lax

D = 256
H = 8
FF = 1024
NC = 128
NBIN = 8
DP = 256
GE = 4
LAYERS = 1
JET_DEV = 16
JETS = 512
N_DP = 4
N_ENS = 32


def draw_counts(key, part):
    raw = jax.random.randint(key, (N_DP, JETS), 4, NC + 1, dtype=jnp.int32)
    position = jnp.arange(JETS, dtype=jnp.int32) % JET_DEV
    return jnp.where(position[None, :] == 0, NC, raw).astype(jnp.int32)


def draw_member(key, part):
    raw = jax.random.randint(jax.random.fold_in(key, 7), (N_DP, N_ENS, JET_DEV), 0, GE, dtype=jnp.int32)
    scores = jax.random.randint(jax.random.fold_in(key, 11), (N_DP, N_ENS, GE), 0, 1 << 20, dtype=jnp.int32)
    scores = scores * GE + jnp.arange(GE, dtype=jnp.int32)
    firsts = jnp.argsort(scores, axis=-1, stable=True).astype(jnp.int32)
    merged = jnp.concatenate([firsts, raw[..., GE:]], axis=-1)
    return merged.reshape(N_DP, JETS).astype(jnp.int32)


def set_ends(values, key, low, top_value):
    index_at = [jax.random.randint(jax.random.fold_in(key, axis), (), 0, length) for axis, length in enumerate(values.shape)]
    longest = values.shape.index(max(values.shape))
    neighbour = index_at[:longest] + [(index_at[longest] + 1) % values.shape[longest]] + index_at[longest + 1:]
    return values.at[tuple(index_at)].set(low).at[tuple(neighbour)].set(top_value)


def shard_levels(own_key, shape, split, smallest, largest):
    def one(dim, parts):
        heights = jax.random.uniform(jax.random.fold_in(jax.random.fold_in(own_key, 6), dim), (parts,), jnp.float32, smallest / len(split), largest / len(split))
        return jnp.repeat(jnp.exp(heights), shape[dim] // parts).reshape((-1,) + (1,) * (len(shape) - dim - 1))

    factor_of = one(*split[0])
    for cut in split[1:]:
        factor_of = factor_of * one(*cut)
    return factor_of


def gaussian(key, extent, spread, most, split=(), kind=jnp.bfloat16):
    level = shard_levels(key, extent, split, -0.22, 0.18) if split else 1.0
    result = jax.random.normal(key, extent, jnp.float32) * spread * level
    return jnp.minimum(jnp.maximum(result, -most), most).astype(kind)


def setup_inputs(seed: int = 0) -> dict:
    arg_keys = jax.random.split(jax.random.key(seed), 16)
    return {
        "embed": gaussian(arg_keys[0], (N_DP, JETS, NC, D), 1.0, 6.0, ((0, 4), (1, 32))),
        "counts": draw_counts(jax.random.fold_in(arg_keys[15], 71), 0),
        "member": draw_member(jax.random.fold_in(arg_keys[15], 71), 0),
        "bins": set_ends(jax.random.randint(arg_keys[3], (N_DP, JETS, NC, NC), 0, NBIN), jax.random.fold_in(arg_keys[3], 1), 0, NBIN - 1).astype(jnp.int32),
        "masses": jnp.clip(jax.random.uniform(arg_keys[4], (N_DP, GE), jnp.float32, -1.5, 1.5) * shard_levels(arg_keys[4], (N_DP, GE), ((0, 4),), -0.4, 0.0), -1.5, 1.5),
        "gain_attn": jnp.clip(1.0 + 0.15 * jax.random.normal(arg_keys[5], (LAYERS, D), jnp.float32), 0.25, 1.75),
        "w_qkv": gaussian(arg_keys[6], (LAYERS, D, 3 * D), D ** -0.5, 0.375),
        "w_out": gaussian(arg_keys[7], (LAYERS, D, D), D ** -0.5, 0.375),
        "pair_table": gaussian(arg_keys[8], (LAYERS, NBIN, H), 1.0, 4.0, (), jnp.float32),
        "gain_ffn": jnp.clip(1.0 + 0.15 * jax.random.normal(arg_keys[9], (LAYERS, D), jnp.float32), 0.25, 1.75),
        "w_up": gaussian(arg_keys[10], (LAYERS, D, FF), D ** -0.5, 0.375),
        "w_down": gaussian(arg_keys[11], (LAYERS, FF, D), FF ** -0.5, 0.1875),
        "w_phi": gaussian(arg_keys[12], (D, DP), D ** -0.5, 0.375),
        "w_mean": gaussian(arg_keys[13], (DP,), DP ** -0.5, 0.375, (), jnp.float32),
        "w_scale": gaussian(arg_keys[14], (DP,), DP ** -0.5, 0.375, (), jnp.float32),
    }


def normalize(stream, gain_vec):
    average = lax.optimization_barrier(jnp.mean(stream, axis=-1, keepdims=True))
    centred = stream - average
    variance = lax.optimization_barrier(jnp.mean(centred * centred, axis=-1, keepdims=True))
    return centred * lax.rsqrt(variance + 1e-05) * gain_vec

def encoder(packed, jets, lengths, pair_bins):
    gain_attn, w_qkv, w_out, pair_table, gain_ffn, w_up, w_down, w_phi = packed
    count_jets, slots, width = jets.shape
    heads = pair_table.shape[2]
    head_dim = width // heads
    live_keys = jnp.arange(slots, dtype=jnp.int32)[None, :] < lengths[:, None]
    bin_onehot = (pair_bins[..., None] == jnp.arange(pair_table.shape[1], dtype=jnp.int32)).astype(jnp.float32)
    stream = jets
    for depth in range(w_qkv.shape[0]):
        pair_bias = jnp.einsum('jqkb,bh->jhqk', bin_onehot, pair_table[depth], precision=lax.Precision.HIGHEST)
        normed = normalize(stream.astype(jnp.float32), gain_attn[depth]).astype(jnp.bfloat16).reshape(count_jets * slots, width)
        projected = jnp.dot(normed, w_qkv[depth], preferred_element_type=jnp.float32).astype(jnp.bfloat16)
        projected = projected.reshape(count_jets, slots, 3, heads, head_dim)
        queries = projected[:, :, 0].astype(jnp.float32)
        key_rows = projected[:, :, 1].astype(jnp.float32)
        value_rows = projected[:, :, 2].astype(jnp.float32)
        scores = jnp.einsum('jqhe,jkhe->jhqk', queries, key_rows) / math.sqrt(head_dim) + pair_bias
        scores = jnp.where(live_keys[:, None, None, :], scores, -1e+30)
        attend = jax.nn.softmax(scores, axis=-1).astype(jnp.bfloat16)
        context = jnp.einsum('jhqk,jkhe->jqhe', attend.astype(jnp.float32), value_rows).astype(jnp.bfloat16)
        context = context.reshape(count_jets * slots, width)
        middle = stream.astype(jnp.float32).reshape(count_jets * slots, width) + jnp.dot(context, w_out[depth], preferred_element_type=jnp.float32)
        normed = normalize(middle, gain_ffn[depth]).astype(jnp.bfloat16)
        hidden = jax.nn.gelu(jnp.dot(normed, w_up[depth], preferred_element_type=jnp.float32)).astype(jnp.bfloat16)
        stream = (middle + jnp.dot(hidden, w_down[depth], preferred_element_type=jnp.float32)).astype(jnp.bfloat16)
        stream = stream.reshape(count_jets, slots, width)
    pooled = lax.optimization_barrier(jnp.sum(jnp.where(live_keys[..., None], stream.astype(jnp.float32), 0.0), axis=1))
    pooled = (pooled / lengths[:, None].astype(jnp.float32)).astype(jnp.bfloat16)
    return jax.nn.gelu(jnp.dot(pooled, w_phi, preferred_element_type=jnp.float32))

def flow_head(head_weights, summed, number, masses):
    w_mean, w_scale = head_weights
    average = summed / number[..., None]
    centre = lax.optimization_barrier(jnp.sum(average * w_mean, axis=-1))
    log_width = lax.optimization_barrier(jnp.sum(average * w_scale, axis=-1))
    return 0.5 * jnp.square((masses - centre) * jnp.exp(-log_width)) + log_width

def reference(embed, counts, member, bins, masses, gain_attn, w_qkv, w_out, pair_table, gain_ffn, w_up, w_down, w_phi, w_mean, w_scale):
    packed = (gain_attn, w_qkv, w_out, pair_table, gain_ffn, w_up, w_down, w_phi)
    blocks = N_DP * N_ENS
    emb_blocks = embed.reshape(blocks, JET_DEV, NC, D)
    count_blocks = counts.reshape(blocks, JET_DEV)
    bin_blocks = bins.reshape(blocks, JET_DEV, NC, NC)

    def forward_block(items):
        return encoder(packed, items[0], items[1], items[2])
    phi_all = lax.map(forward_block, (emb_blocks, count_blocks, bin_blocks))
    phi_all = phi_all.reshape(N_DP, N_ENS, JET_DEV, DP)
    group_onehot = (member.reshape(N_DP, N_ENS, JET_DEV)[..., None] == jnp.arange(GE, dtype=jnp.int32)).astype(jnp.float32)
    summed = jnp.einsum('gnje,gnjp->gep', group_onehot, phi_all, precision=lax.Precision.HIGHEST)
    number = lax.optimization_barrier(jnp.sum(group_onehot, axis=(1, 2)))

    def head_part(head_weights, summed_in):
        return flow_head(head_weights, summed_in, number, masses)
    neg_loglik, back_head = jax.vjp(head_part, (w_mean, w_scale), summed)
    head_grads, summed_grad = back_head(jnp.full(neg_loglik.shape, 1.0 / (N_DP * GE), jnp.float32))
    phi_grad = jnp.einsum('gnje,gep->gnjp', group_onehot, summed_grad, precision=lax.Precision.HIGHEST)
    phi_grad = phi_grad.reshape(blocks, JET_DEV, DP)

    def backward_block(carry, items):

        def local_part(params_in):
            return encoder(params_in, items[0], items[1], items[2])
        unused, back_trunk = jax.vjp(local_part, packed)
        partial_grads = back_trunk(items[3])[0]
        return (jax.tree.map(lambda total, piece: total + piece.astype(jnp.float32), carry, partial_grads), None)
    start = jax.tree.map(lambda weight_arr: jnp.zeros(weight_arr.shape, jnp.float32), packed)
    grads, unused = lax.scan(backward_block, start, (emb_blocks, count_blocks, bin_blocks, phi_grad))
    return (neg_loglik, grads[0], grads[1], grads[2], grads[3], grads[4], grads[5], grads[6], grads[7], head_grads[0], head_grads[1])
```

```python
import math

import jax
import jax.numpy as jnp
from jax import lax
from jax.sharding import PartitionSpec as P


def normalize(stream, gain_vec):
    average = jnp.mean(stream, axis=-1, keepdims=True)
    centred = stream - average
    variance = jnp.mean(centred * centred, axis=-1, keepdims=True)
    return centred * lax.rsqrt(variance + 1e-05) * gain_vec


def encoder(packed, jets, lengths, pair_bins):
    gain_attn, w_qkv, w_out, pair_table, gain_ffn, w_up, w_down, w_phi = packed
    count_jets, slots, width = jets.shape
    heads = pair_table.shape[2]
    head_dim = width // heads
    live_keys = jnp.arange(slots, dtype=jnp.int32)[None, :] < lengths[:, None]
    bin_onehot = (pair_bins[..., None] == jnp.arange(pair_table.shape[1], dtype=jnp.int32)).astype(
        jnp.float32
    )
    stream = jets
    pair_bias = jnp.einsum(
        "jqkb,bh->jhqk", bin_onehot, pair_table[0], precision=lax.Precision.HIGHEST
    )
    normed = (
        normalize(stream.astype(jnp.float32), gain_attn[0])
        .astype(jnp.bfloat16)
        .reshape(count_jets * slots, width)
    )
    projected = jnp.dot(normed, w_qkv[0], preferred_element_type=jnp.float32).astype(jnp.bfloat16)
    projected = projected.reshape(count_jets, slots, 3, heads, head_dim)
    queries = projected[:, :, 0]
    key_rows = projected[:, :, 1]
    value_rows = projected[:, :, 2]
    scores = (
        jnp.einsum("jqhe,jkhe->jhqk", queries, key_rows, preferred_element_type=jnp.float32)
        / math.sqrt(head_dim)
        + pair_bias
    )
    scores = jnp.where(live_keys[:, None, None, :], scores, -1e30)
    attend = jax.nn.softmax(scores, axis=-1).astype(jnp.bfloat16)
    context = jnp.einsum(
        "jhqk,jkhe->jqhe", attend, value_rows, preferred_element_type=jnp.float32
    ).astype(jnp.bfloat16)
    context = context.reshape(count_jets * slots, width)
    middle = stream.astype(jnp.float32).reshape(count_jets * slots, width) + jnp.dot(
        context, w_out[0], preferred_element_type=jnp.float32
    )
    normed = normalize(middle, gain_ffn[0]).astype(jnp.bfloat16)
    hidden = jax.nn.gelu(jnp.dot(normed, w_up[0], preferred_element_type=jnp.float32)).astype(
        jnp.bfloat16
    )
    stream = (middle + jnp.dot(hidden, w_down[0], preferred_element_type=jnp.float32)).astype(
        jnp.bfloat16
    )
    stream = stream.reshape(count_jets, slots, width)
    pooled = jnp.sum(jnp.where(live_keys[..., None], stream.astype(jnp.float32), 0.0), axis=1)
    pooled = (pooled / lengths[:, None].astype(jnp.float32)).astype(jnp.bfloat16)
    return jax.nn.gelu(jnp.dot(pooled, w_phi, preferred_element_type=jnp.float32))


def flow_head(head_weights, summed, number, masses):
    w_mean, w_scale = head_weights
    average = summed / number[..., None]
    centre = jnp.sum(average * w_mean, axis=-1)
    log_width = jnp.sum(average * w_scale, axis=-1)
    return 0.5 * jnp.square((masses - centre) * jnp.exp(-log_width)) + log_width


def butterfly_sum(value, axis, size):
    step = 1
    while step < size:
        pairs = [(index, index ^ step) for index in range(size)]
        value = value + lax.ppermute(value, axis, pairs)
        step *= 2
    return value


def shards(
    embed,
    counts,
    member,
    bins,
    masses,
    gain_attn,
    w_qkv,
    w_out,
    pair_table,
    gain_ffn,
    w_up,
    w_down,
    w_phi,
    w_mean,
    w_scale,
):
    packed = (gain_attn, w_qkv, w_out, pair_table, gain_ffn, w_up, w_down, w_phi)
    jets = embed[0]
    lengths = counts[0]
    pair_bins = bins[0]
    group_masses = masses[0]
    groups_total = group_masses.shape[0]
    width = w_phi.shape[1]

    def local_part(params_in):
        return encoder(params_in, jets, lengths, pair_bins)

    phi, back_trunk = jax.vjp(local_part, packed)
    group_onehot = (member[0][:, None] == jnp.arange(groups_total, dtype=jnp.int32)).astype(
        jnp.float32
    )
    partial_sum = jnp.dot(group_onehot.T, phi, precision=lax.Precision.HIGHEST)
    tally = jnp.sum(group_onehot, axis=0)
    stacked = jnp.concatenate(
        [partial_sum, jnp.zeros((1, width), jnp.float32).at[0, :groups_total].set(tally)], axis=0
    )
    stacked = butterfly_sum(stacked, "ens", lax.axis_size("ens"))
    summed = stacked[:groups_total]
    number = stacked[groups_total, :groups_total]

    def head_part(head_weights, summed_in):
        return flow_head(head_weights, summed_in, number, group_masses)

    neg_loglik, back_head = jax.vjp(head_part, (w_mean, w_scale), summed)
    scale_total = 1.0 / (lax.axis_size("dp") * groups_total)
    head_grads, summed_grad = back_head(jnp.full(neg_loglik.shape, scale_total, jnp.float32))
    phi_grad = jnp.dot(group_onehot, summed_grad, precision=lax.Precision.HIGHEST)
    partial_grads = [piece.astype(jnp.float32) for piece in back_trunk(phi_grad)[0]]
    first = (lax.axis_index("ens") == 0).astype(jnp.float32)
    misc = jnp.zeros((8, width), jnp.float32)
    misc = misc.at[0].set(partial_grads[0][0])
    misc = misc.at[1].set(partial_grads[4][0])
    misc = misc.at[2].set(head_grads[0] * first)
    misc = misc.at[3].set(head_grads[1] * first)
    table_size = partial_grads[3].size
    misc = misc.at[4, :table_size].set(partial_grads[3].reshape(-1))
    phi_rows = partial_grads[7].shape[0]
    tail = jnp.concatenate([partial_grads[7], misc], axis=0)
    totals = lax.psum(
        (
            partial_grads[1],
            partial_grads[2],
            partial_grads[5],
            partial_grads[6],
            tail,
        ),
        ("dp", "ens"),
    )
    grad_qkv, grad_out, grad_up, grad_down, tail = totals
    grad_phi = tail[:phi_rows]
    misc = tail[phi_rows:]
    return (
        neg_loglik[None, :],
        misc[0][None, :],
        grad_qkv,
        grad_out,
        misc[4, :table_size].reshape(partial_grads[3].shape),
        misc[1][None, :],
        grad_up,
        grad_down,
        grad_phi,
        misc[2],
        misc[3],
    )


def solution(mesh):
    in_specs = (
        P("dp", "ens", None, None),
        P("dp", "ens"),
        P("dp", "ens"),
        P("dp", "ens", None, None),
        P("dp", None),
        P(),
        P(),
        P(),
        P(),
        P(),
        P(),
        P(),
        P(),
        P(),
        P(),
    )
    out_specs = (P("dp", None), P(), P(), P(), P(), P(), P(), P(), P(), P(), P())
    return jax.shard_map(shards, mesh=mesh, in_specs=in_specs, out_specs=out_specs, check_vma=False)
```

```python
import math

import jax
import jax.numpy as jnp
from jax import lax
from jax.sharding import PartitionSpec as P


def normalize(stream, gain_vec):
    average = jnp.mean(stream, axis=-1, keepdims=True)
    centred = stream - average
    variance = jnp.mean(centred * centred, axis=-1, keepdims=True)
    return centred * lax.rsqrt(variance + 1e-05) * gain_vec


def encoder(packed, jets, lengths, pair_bins):
    gain_attn, w_qkv, w_out, pair_table, gain_ffn, w_up, w_down, w_phi = packed
    count_jets, slots, width = jets.shape
    heads = pair_table.shape[2]
    head_dim = width // heads
    live_keys = jnp.arange(slots, dtype=jnp.int32)[None, :] < lengths[:, None]
    bin_onehot = (pair_bins[..., None] == jnp.arange(pair_table.shape[1], dtype=jnp.int32)).astype(
        jnp.float32
    )
    stream = jets
    pair_bias = jnp.einsum(
        "jqkb,bh->jhqk", bin_onehot, pair_table[0], precision=lax.Precision.HIGHEST
    )
    normed = (
        normalize(stream.astype(jnp.float32), gain_attn[0])
        .astype(jnp.bfloat16)
        .reshape(count_jets * slots, width)
    )
    projected = jnp.dot(normed, w_qkv[0], preferred_element_type=jnp.float32).astype(jnp.bfloat16)
    projected = projected.reshape(count_jets, slots, 3, heads, head_dim)
    queries = projected[:, :, 0]
    key_rows = projected[:, :, 1]
    value_rows = projected[:, :, 2]
    scores = (
        jnp.einsum("jqhe,jkhe->jhqk", queries, key_rows, preferred_element_type=jnp.float32)
        / math.sqrt(head_dim)
        + pair_bias
    )
    scores = jnp.where(live_keys[:, None, None, :], scores, -1e30)
    attend = jax.nn.softmax(scores, axis=-1).astype(jnp.bfloat16)
    context = jnp.einsum(
        "jhqk,jkhe->jqhe", attend, value_rows, preferred_element_type=jnp.float32
    ).astype(jnp.bfloat16)
    context = context.reshape(count_jets * slots, width)
    middle = stream.astype(jnp.float32).reshape(count_jets * slots, width) + jnp.dot(
        context, w_out[0], preferred_element_type=jnp.float32
    )
    normed = normalize(middle, gain_ffn[0]).astype(jnp.bfloat16)
    hidden = jax.nn.gelu(jnp.dot(normed, w_up[0], preferred_element_type=jnp.float32)).astype(
        jnp.bfloat16
    )
    stream = (middle + jnp.dot(hidden, w_down[0], preferred_element_type=jnp.float32)).astype(
        jnp.bfloat16
    )
    stream = stream.reshape(count_jets, slots, width)
    pooled = jnp.sum(jnp.where(live_keys[..., None], stream.astype(jnp.float32), 0.0), axis=1)
    pooled = (pooled / lengths[:, None].astype(jnp.float32)).astype(jnp.bfloat16)
    return jax.nn.gelu(jnp.dot(pooled, w_phi, preferred_element_type=jnp.float32))


def flow_head(head_weights, summed, number, masses):
    w_mean, w_scale = head_weights
    average = summed / number[..., None]
    centre = jnp.sum(average * w_mean, axis=-1)
    log_width = jnp.sum(average * w_scale, axis=-1)
    return 0.5 * jnp.square((masses - centre) * jnp.exp(-log_width)) + log_width


def butterfly_sum(value, axis, size):
    step = 1
    while step < size:
        pairs = [(index, index ^ step) for index in range(size)]
        value = value + lax.ppermute(value, axis, pairs)
        step *= 2
    return value


def halving_steps(mesh_sizes):
    steps = []
    for axis, size in mesh_sizes:
        step = 1
        while step < size:
            steps.append((axis, step))
            step *= 2
    return steps


def halve_sum(buffer, axis, step):
    rows = buffer.shape[0] // 2
    side = (lax.axis_index(axis) // step) % 2
    keep = lax.dynamic_slice_in_dim(buffer, side * rows, rows, 0)
    send = lax.dynamic_slice_in_dim(buffer, (1 - side) * rows, rows, 0)
    size = lax.axis_size(axis)
    pairs = [(index, index ^ step) for index in range(size)]
    return keep + lax.ppermute(send, axis, pairs)


def double_gather(buffer, axis, step):
    rows = buffer.shape[0]
    side = (lax.axis_index(axis) // step) % 2
    size = lax.axis_size(axis)
    pairs = [(index, index ^ step) for index in range(size)]
    other = lax.ppermute(buffer, axis, pairs)
    whole = jnp.zeros((2 * rows,) + buffer.shape[1:], buffer.dtype)
    whole = lax.dynamic_update_slice_in_dim(whole, buffer, side * rows, 0)
    return lax.dynamic_update_slice_in_dim(whole, other, (1 - side) * rows, 0)


def ring_all_reduce(buffer, steps):
    for axis, step in steps:
        buffer = halve_sum(buffer, axis, step)
    for axis, step in reversed(steps):
        buffer = double_gather(buffer, axis, step)
    return buffer


def shards(
    embed,
    counts,
    member,
    bins,
    masses,
    gain_attn,
    w_qkv,
    w_out,
    pair_table,
    gain_ffn,
    w_up,
    w_down,
    w_phi,
    w_mean,
    w_scale,
):
    packed = (gain_attn, w_qkv, w_out, pair_table, gain_ffn, w_up, w_down, w_phi)
    jets = embed[0]
    lengths = counts[0]
    pair_bins = bins[0]
    group_masses = masses[0]
    groups_total = group_masses.shape[0]
    width = w_phi.shape[1]

    def local_part(params_in):
        return encoder(params_in, jets, lengths, pair_bins)

    phi, back_trunk = jax.vjp(local_part, packed)
    group_onehot = (member[0][:, None] == jnp.arange(groups_total, dtype=jnp.int32)).astype(
        jnp.float32
    )
    partial_sum = jnp.dot(group_onehot.T, phi, precision=lax.Precision.HIGHEST)
    tally = jnp.sum(group_onehot, axis=0)
    stacked = jnp.concatenate(
        [partial_sum, jnp.zeros((1, width), jnp.float32).at[0, :groups_total].set(tally)], axis=0
    )
    stacked = butterfly_sum(stacked, "ens", lax.axis_size("ens"))
    summed = stacked[:groups_total]
    number = stacked[groups_total, :groups_total]

    def head_part(head_weights, summed_in):
        return flow_head(head_weights, summed_in, number, group_masses)

    neg_loglik, back_head = jax.vjp(head_part, (w_mean, w_scale), summed)
    scale_total = 1.0 / (lax.axis_size("dp") * groups_total)
    head_grads, summed_grad = back_head(jnp.full(neg_loglik.shape, scale_total, jnp.float32))
    phi_grad = jnp.dot(group_onehot, summed_grad, precision=lax.Precision.HIGHEST)
    partial_grads = [piece.astype(jnp.float32) for piece in back_trunk(phi_grad)[0]]
    first = (lax.axis_index("ens") == 0).astype(jnp.float32)
    misc = jnp.zeros((8, width), jnp.float32)
    misc = misc.at[0].set(partial_grads[0][0])
    misc = misc.at[1].set(partial_grads[4][0])
    misc = misc.at[2].set(head_grads[0] * first)
    misc = misc.at[3].set(head_grads[1] * first)
    table_size = partial_grads[3].size
    misc = misc.at[4, :table_size].set(partial_grads[3].reshape(-1))
    pieces = [partial_grads[1], partial_grads[2], partial_grads[5], partial_grads[6], partial_grads[7], misc]
    flat = [piece.reshape(-1, width) for piece in pieces]
    offsets = [0]
    for piece in flat:
        offsets.append(offsets[-1] + piece.shape[0])
    steps = halving_steps((("dp", lax.axis_size("dp")), ("ens", lax.axis_size("ens"))))
    quantum = 8 << len(steps)
    padded = -(-offsets[-1] // quantum) * quantum
    flat.append(jnp.zeros((padded - offsets[-1], width), jnp.float32))
    reduced = ring_all_reduce(jnp.concatenate(flat, axis=0), steps)
    grad_qkv, grad_out, grad_up, grad_down, grad_phi, misc = [
        reduced[offsets[k] : offsets[k + 1]].reshape(pieces[k].shape) for k in range(len(pieces))
    ]
    return (
        neg_loglik[None, :],
        misc[0][None, :],
        grad_qkv,
        grad_out,
        misc[4, :table_size].reshape(partial_grads[3].shape),
        misc[1][None, :],
        grad_up,
        grad_down,
        grad_phi,
        misc[2],
        misc[3],
    )


def solution(mesh):
    in_specs = (
        P("dp", "ens", None, None),
        P("dp", "ens"),
        P("dp", "ens"),
        P("dp", "ens", None, None),
        P("dp", None),
        P(),
        P(),
        P(),
        P(),
        P(),
        P(),
        P(),
        P(),
        P(),
        P(),
    )
    out_specs = (P("dp", None), P(), P(), P(), P(), P(), P(), P(), P(), P(), P())
    return jax.shard_map(shards, mesh=mesh, in_specs=in_specs, out_specs=out_specs, check_vma=False)
```

```python
import math

import jax
import jax.numpy as jnp
from jax import lax
from jax.sharding import PartitionSpec as P


def normalize(stream, gain_vec):
    average = jnp.mean(stream, axis=-1, keepdims=True)
    centred = stream - average
    variance = jnp.mean(centred * centred, axis=-1, keepdims=True)
    return centred * lax.rsqrt(variance + 1e-05) * gain_vec


def encoder(packed, jets, lengths, pair_bins):
    gain_attn, w_qkv, w_out, pair_table, gain_ffn, w_up, w_down, w_phi = packed
    count_jets, slots, width = jets.shape
    heads = pair_table.shape[2]
    head_dim = width // heads
    live_keys = jnp.arange(slots, dtype=jnp.int32)[None, :] < lengths[:, None]
    bin_onehot = (pair_bins[..., None] == jnp.arange(pair_table.shape[1], dtype=jnp.int32)).astype(
        jnp.float32
    )
    stream = jets
    pair_bias = jnp.einsum(
        "jqkb,bh->jhqk", bin_onehot, pair_table[0], precision=lax.Precision.HIGHEST
    )
    normed = (
        normalize(stream.astype(jnp.float32), gain_attn[0])
        .astype(jnp.bfloat16)
        .reshape(count_jets * slots, width)
    )
    projected = jnp.dot(normed, w_qkv[0], preferred_element_type=jnp.float32).astype(jnp.bfloat16)
    projected = projected.reshape(count_jets, slots, 3, heads, head_dim)
    queries = projected[:, :, 0]
    key_rows = projected[:, :, 1]
    value_rows = projected[:, :, 2]
    scores = (
        jnp.einsum("jqhe,jkhe->jhqk", queries, key_rows, preferred_element_type=jnp.float32)
        / math.sqrt(head_dim)
        + pair_bias
    )
    scores = jnp.where(live_keys[:, None, None, :], scores, -1e30)
    attend = jax.nn.softmax(scores, axis=-1).astype(jnp.bfloat16)
    context = jnp.einsum(
        "jhqk,jkhe->jqhe", attend, value_rows, preferred_element_type=jnp.float32
    ).astype(jnp.bfloat16)
    context = context.reshape(count_jets * slots, width)
    middle = stream.astype(jnp.float32).reshape(count_jets * slots, width) + jnp.dot(
        context, w_out[0], preferred_element_type=jnp.float32
    )
    normed = normalize(middle, gain_ffn[0]).astype(jnp.bfloat16)
    hidden = jax.nn.gelu(jnp.dot(normed, w_up[0], preferred_element_type=jnp.float32)).astype(
        jnp.bfloat16
    )
    stream = (middle + jnp.dot(hidden, w_down[0], preferred_element_type=jnp.float32)).astype(
        jnp.bfloat16
    )
    stream = stream.reshape(count_jets, slots, width)
    pooled = jnp.sum(jnp.where(live_keys[..., None], stream.astype(jnp.float32), 0.0), axis=1)
    pooled = (pooled / lengths[:, None].astype(jnp.float32)).astype(jnp.bfloat16)
    return jax.nn.gelu(jnp.dot(pooled, w_phi, preferred_element_type=jnp.float32))


def flow_head(head_weights, summed, number, masses):
    w_mean, w_scale = head_weights
    average = summed / number[..., None]
    centre = jnp.sum(average * w_mean, axis=-1)
    log_width = jnp.sum(average * w_scale, axis=-1)
    return 0.5 * jnp.square((masses - centre) * jnp.exp(-log_width)) + log_width


def butterfly_sum(value, axis, size):
    step = 1
    while step < size:
        pairs = [(index, index ^ step) for index in range(size)]
        value = value + lax.ppermute(value, axis, pairs)
        step *= 2
    return value


def halving_steps(mesh_sizes):
    steps = []
    for axis, size in mesh_sizes:
        step = 1
        while step < size:
            steps.append((axis, step))
            step *= 2
    return steps


def halve_sum(buffer, axis, step):
    rows = buffer.shape[0] // 2
    side = (lax.axis_index(axis) // step) % 2
    keep = lax.dynamic_slice_in_dim(buffer, side * rows, rows, 0)
    send = lax.dynamic_slice_in_dim(buffer, (1 - side) * rows, rows, 0)
    size = lax.axis_size(axis)
    pairs = [(index, index ^ step) for index in range(size)]
    return keep + lax.ppermute(send, axis, pairs)


def double_gather(buffer, axis, step):
    rows = buffer.shape[0]
    side = (lax.axis_index(axis) // step) % 2
    size = lax.axis_size(axis)
    pairs = [(index, index ^ step) for index in range(size)]
    other = lax.ppermute(buffer, axis, pairs)
    whole = jnp.zeros((2 * rows,) + buffer.shape[1:], buffer.dtype)
    whole = lax.dynamic_update_slice_in_dim(whole, buffer, side * rows, 0)
    return lax.dynamic_update_slice_in_dim(whole, other, (1 - side) * rows, 0)


def ring_all_reduce(buffer, first, orders):
    buffer = halve_sum(buffer, *first)
    colors = jnp.split(buffer, len(orders), axis=0)
    for step_index in range(len(orders[0])):
        colors = [halve_sum(part, *order[step_index]) for part, order in zip(colors, orders)]
    for step_index in reversed(range(len(orders[0]))):
        colors = [double_gather(part, *order[step_index]) for part, order in zip(colors, orders)]
    return double_gather(jnp.concatenate(colors, axis=0), *first)


def shards(
    embed,
    counts,
    member,
    bins,
    masses,
    gain_attn,
    w_qkv,
    w_out,
    pair_table,
    gain_ffn,
    w_up,
    w_down,
    w_phi,
    w_mean,
    w_scale,
):
    packed = (gain_attn, w_qkv, w_out, pair_table, gain_ffn, w_up, w_down, w_phi)
    jets = embed[0]
    lengths = counts[0]
    pair_bins = bins[0]
    group_masses = masses[0]
    groups_total = group_masses.shape[0]
    width = w_phi.shape[1]

    def local_part(params_in):
        return encoder(params_in, jets, lengths, pair_bins)

    phi, back_trunk = jax.vjp(local_part, packed)
    group_onehot = (member[0][:, None] == jnp.arange(groups_total, dtype=jnp.int32)).astype(
        jnp.float32
    )
    partial_sum = jnp.dot(group_onehot.T, phi, precision=lax.Precision.HIGHEST)
    tally = jnp.sum(group_onehot, axis=0)
    stacked = jnp.concatenate(
        [partial_sum, jnp.zeros((1, width), jnp.float32).at[0, :groups_total].set(tally)], axis=0
    )
    stacked = butterfly_sum(stacked, "ens", lax.axis_size("ens"))
    summed = stacked[:groups_total]
    number = stacked[groups_total, :groups_total]

    def head_part(head_weights, summed_in):
        return flow_head(head_weights, summed_in, number, group_masses)

    neg_loglik, back_head = jax.vjp(head_part, (w_mean, w_scale), summed)
    scale_total = 1.0 / (lax.axis_size("dp") * groups_total)
    head_grads, summed_grad = back_head(jnp.full(neg_loglik.shape, scale_total, jnp.float32))
    phi_grad = jnp.dot(group_onehot, summed_grad, precision=lax.Precision.HIGHEST)
    partial_grads = [piece.astype(jnp.float32) for piece in back_trunk(phi_grad)[0]]
    first = (lax.axis_index("ens") == 0).astype(jnp.float32)
    misc = jnp.zeros((8, width), jnp.float32)
    misc = misc.at[0].set(partial_grads[0][0])
    misc = misc.at[1].set(partial_grads[4][0])
    misc = misc.at[2].set(head_grads[0] * first)
    misc = misc.at[3].set(head_grads[1] * first)
    table_size = partial_grads[3].size
    misc = misc.at[4, :table_size].set(partial_grads[3].reshape(-1))
    pieces = [partial_grads[1], partial_grads[2], partial_grads[5], partial_grads[6], partial_grads[7], misc]
    flat = [piece.reshape(-1, width) for piece in pieces]
    offsets = [0]
    for piece in flat:
        offsets.append(offsets[-1] + piece.shape[0])
    steps = halving_steps((("dp", lax.axis_size("dp")), ("ens", lax.axis_size("ens"))))
    first, rest = steps[0], steps[1:]
    near = [("dp", 2), ("ens", 1), ("ens", 4)]
    far = [("ens", 16), ("ens", 2), ("ens", 8)]
    assert sorted(near + far) == sorted(rest)
    count = len(near)
    orders = [near[c:] + near[:c] + far[c:] + far[:c] for c in range(count)]
    quantum = 2 * count << len(rest)
    padded = -(-offsets[-1] // quantum) * quantum
    flat.append(jnp.zeros((padded - offsets[-1], width), jnp.float32))
    reduced = ring_all_reduce(jnp.concatenate(flat, axis=0), first, orders)
    grad_qkv, grad_out, grad_up, grad_down, grad_phi, misc = [
        reduced[offsets[k] : offsets[k + 1]].reshape(pieces[k].shape) for k in range(len(pieces))
    ]
    return (
        neg_loglik[None, :],
        misc[0][None, :],
        grad_qkv,
        grad_out,
        misc[4, :table_size].reshape(partial_grads[3].shape),
        misc[1][None, :],
        grad_up,
        grad_down,
        grad_phi,
        misc[2],
        misc[3],
    )


def solution(mesh):
    in_specs = (
        P("dp", "ens", None, None),
        P("dp", "ens"),
        P("dp", "ens"),
        P("dp", "ens", None, None),
        P("dp", None),
        P(),
        P(),
        P(),
        P(),
        P(),
        P(),
        P(),
        P(),
        P(),
        P(),
    )
    out_specs = (P("dp", None), P(), P(), P(), P(), P(), P(), P(), P(), P(), P())
    return jax.shard_map(shards, mesh=mesh, in_specs=in_specs, out_specs=out_specs, check_vma=False)
```

```python
import math

import jax
import jax.numpy as jnp
from jax import lax
from jax.sharding import PartitionSpec as P


def normalize(stream, gain_vec):
    average = jnp.mean(stream, axis=-1, keepdims=True)
    centred = stream - average
    variance = jnp.mean(centred * centred, axis=-1, keepdims=True)
    return centred * lax.rsqrt(variance + 1e-05) * gain_vec


def encoder(packed, jets, lengths, pair_bins):
    gain_attn, w_qkv, w_out, pair_table, gain_ffn, w_up, w_down, w_phi = packed
    count_jets, slots, width = jets.shape
    heads = pair_table.shape[2]
    head_dim = width // heads
    live_keys = jnp.arange(slots, dtype=jnp.int32)[None, :] < lengths[:, None]
    bin_onehot = (pair_bins[..., None] == jnp.arange(pair_table.shape[1], dtype=jnp.int32)).astype(
        jnp.float32
    )
    stream = jets
    pair_bias = jnp.einsum(
        "jqkb,bh->jhqk", bin_onehot, pair_table[0], precision=lax.Precision.HIGHEST
    )
    normed = (
        normalize(stream.astype(jnp.float32), gain_attn[0])
        .astype(jnp.bfloat16)
        .reshape(count_jets * slots, width)
    )
    projected = jnp.dot(normed, w_qkv[0], preferred_element_type=jnp.float32).astype(jnp.bfloat16)
    projected = projected.reshape(count_jets, slots, 3, heads, head_dim)
    queries = projected[:, :, 0]
    key_rows = projected[:, :, 1]
    value_rows = projected[:, :, 2]
    scores = (
        jnp.einsum("jqhe,jkhe->jhqk", queries, key_rows, preferred_element_type=jnp.float32)
        / math.sqrt(head_dim)
        + pair_bias
    )
    scores = jnp.where(live_keys[:, None, None, :], scores, -1e30)
    attend = jax.nn.softmax(scores, axis=-1).astype(jnp.bfloat16)
    context = jnp.einsum(
        "jhqk,jkhe->jqhe", attend, value_rows, preferred_element_type=jnp.float32
    ).astype(jnp.bfloat16)
    context = context.reshape(count_jets * slots, width)
    middle = stream.astype(jnp.float32).reshape(count_jets * slots, width) + jnp.dot(
        context, w_out[0], preferred_element_type=jnp.float32
    )
    normed = normalize(middle, gain_ffn[0]).astype(jnp.bfloat16)
    hidden = jax.nn.gelu(jnp.dot(normed, w_up[0], preferred_element_type=jnp.float32)).astype(
        jnp.bfloat16
    )
    stream = (middle + jnp.dot(hidden, w_down[0], preferred_element_type=jnp.float32)).astype(
        jnp.bfloat16
    )
    stream = stream.reshape(count_jets, slots, width)
    pooled = jnp.sum(jnp.where(live_keys[..., None], stream.astype(jnp.float32), 0.0), axis=1)
    pooled = (pooled / lengths[:, None].astype(jnp.float32)).astype(jnp.bfloat16)
    return jax.nn.gelu(jnp.dot(pooled, w_phi, preferred_element_type=jnp.float32))


def flow_head(head_weights, summed, number, masses):
    w_mean, w_scale = head_weights
    average = summed / number[..., None]
    centre = jnp.sum(average * w_mean, axis=-1)
    log_width = jnp.sum(average * w_scale, axis=-1)
    return 0.5 * jnp.square((masses - centre) * jnp.exp(-log_width)) + log_width


def butterfly_sum(value, axis, size):
    step = 1
    while step < size:
        pairs = [(index, index ^ step) for index in range(size)]
        value = value + lax.ppermute(value, axis, pairs)
        step *= 2
    return value


def halving_steps(mesh_sizes):
    steps = []
    for axis, size in mesh_sizes:
        step = 1
        while step < size:
            steps.append((axis, step))
            step *= 2
    return steps


def halve_sum(buffer, axis, step, dim=0):
    rows = buffer.shape[dim] // 2
    side = (lax.axis_index(axis) // step) % 2
    keep = lax.dynamic_slice_in_dim(buffer, side * rows, rows, dim)
    send = lax.dynamic_slice_in_dim(buffer, (1 - side) * rows, rows, dim)
    size = lax.axis_size(axis)
    pairs = [(index, index ^ step) for index in range(size)]
    return keep + lax.ppermute(send, axis, pairs)


def double_gather(buffer, axis, step, dim=0):
    rows = buffer.shape[dim]
    side = (lax.axis_index(axis) // step) % 2
    size = lax.axis_size(axis)
    pairs = [(index, index ^ step) for index in range(size)]
    other = lax.ppermute(buffer, axis, pairs)
    shape = list(buffer.shape)
    shape[dim] = 2 * rows
    whole = jnp.zeros(shape, buffer.dtype)
    whole = lax.dynamic_update_slice_in_dim(whole, buffer, side * rows, dim)
    return lax.dynamic_update_slice_in_dim(whole, other, (1 - side) * rows, dim)


def ring_all_reduce(buffer, first, orders, common):
    buffer = halve_sum(buffer, *first)
    colors = jnp.split(buffer, len(orders), axis=0)
    for step_index in range(len(orders[0])):
        colors = [halve_sum(part, *order[step_index]) for part, order in zip(colors, orders)]
    stacked = jnp.stack(colors)
    for axis, step in common:
        stacked = halve_sum(stacked, axis, step, dim=1)
    for axis, step in reversed(common):
        stacked = double_gather(stacked, axis, step, dim=1)
    colors = [stacked[k] for k in range(len(orders))]
    for step_index in reversed(range(len(orders[0]))):
        colors = [double_gather(part, *order[step_index]) for part, order in zip(colors, orders)]
    return double_gather(jnp.concatenate(colors, axis=0), *first)


def shards(
    embed,
    counts,
    member,
    bins,
    masses,
    gain_attn,
    w_qkv,
    w_out,
    pair_table,
    gain_ffn,
    w_up,
    w_down,
    w_phi,
    w_mean,
    w_scale,
):
    packed = (gain_attn, w_qkv, w_out, pair_table, gain_ffn, w_up, w_down, w_phi)
    jets = embed[0]
    lengths = counts[0]
    pair_bins = bins[0]
    group_masses = masses[0]
    groups_total = group_masses.shape[0]
    width = w_phi.shape[1]

    def local_part(params_in):
        return encoder(params_in, jets, lengths, pair_bins)

    phi, back_trunk = jax.vjp(local_part, packed)
    group_onehot = (member[0][:, None] == jnp.arange(groups_total, dtype=jnp.int32)).astype(
        jnp.float32
    )
    partial_sum = jnp.dot(group_onehot.T, phi, precision=lax.Precision.HIGHEST)
    tally = jnp.sum(group_onehot, axis=0)
    stacked = jnp.concatenate(
        [partial_sum, jnp.zeros((1, width), jnp.float32).at[0, :groups_total].set(tally)], axis=0
    )
    stacked = butterfly_sum(stacked, "ens", lax.axis_size("ens"))
    summed = stacked[:groups_total]
    number = stacked[groups_total, :groups_total]

    def head_part(head_weights, summed_in):
        return flow_head(head_weights, summed_in, number, group_masses)

    neg_loglik, back_head = jax.vjp(head_part, (w_mean, w_scale), summed)
    scale_total = 1.0 / (lax.axis_size("dp") * groups_total)
    head_grads, summed_grad = back_head(jnp.full(neg_loglik.shape, scale_total, jnp.float32))
    phi_grad = jnp.dot(group_onehot, summed_grad, precision=lax.Precision.HIGHEST)
    partial_grads = [piece.astype(jnp.float32) for piece in back_trunk(phi_grad)[0]]
    first = (lax.axis_index("ens") == 0).astype(jnp.float32)
    misc = jnp.zeros((8, width), jnp.float32)
    misc = misc.at[0].set(partial_grads[0][0])
    misc = misc.at[1].set(partial_grads[4][0])
    misc = misc.at[2].set(head_grads[0] * first)
    misc = misc.at[3].set(head_grads[1] * first)
    table_size = partial_grads[3].size
    misc = misc.at[4, :table_size].set(partial_grads[3].reshape(-1))
    pieces = [partial_grads[1], partial_grads[2], partial_grads[5], partial_grads[6], partial_grads[7], misc]
    flat = [piece.reshape(-1, width) for piece in pieces]
    offsets = [0]
    for piece in flat:
        offsets.append(offsets[-1] + piece.shape[0])
    steps = halving_steps((("dp", lax.axis_size("dp")), ("ens", lax.axis_size("ens"))))
    first, rest = steps[0], steps[1:]
    near = [("dp", 2), ("ens", 1), ("ens", 4)]
    far = [("ens", 16), ("ens", 2), ("ens", 8)]
    assert sorted(near + far) == sorted(rest)
    count = len(near)
    orders = [near[c:] + near[:c] for c in range(count)]
    quantum = 2 * count << len(rest)
    padded = -(-offsets[-1] // quantum) * quantum
    flat.append(jnp.zeros((padded - offsets[-1], width), jnp.float32))
    reduced = ring_all_reduce(jnp.concatenate(flat, axis=0), first, orders, far)
    grad_qkv, grad_out, grad_up, grad_down, grad_phi, misc = [
        reduced[offsets[k] : offsets[k + 1]].reshape(pieces[k].shape) for k in range(len(pieces))
    ]
    return (
        neg_loglik[None, :],
        misc[0][None, :],
        grad_qkv,
        grad_out,
        misc[4, :table_size].reshape(partial_grads[3].shape),
        misc[1][None, :],
        grad_up,
        grad_down,
        grad_phi,
        misc[2],
        misc[3],
    )


def solution(mesh):
    in_specs = (
        P("dp", "ens", None, None),
        P("dp", "ens"),
        P("dp", "ens"),
        P("dp", "ens", None, None),
        P("dp", None),
        P(),
        P(),
        P(),
        P(),
        P(),
        P(),
        P(),
        P(),
        P(),
        P(),
    )
    out_specs = (P("dp", None), P(), P(), P(), P(), P(), P(), P(), P(), P(), P())
    return jax.shard_map(shards, mesh=mesh, in_specs=in_specs, out_specs=out_specs, check_vma=False)
```

```python
import math

import jax
import jax.numpy as jnp
from jax import lax
from jax.sharding import PartitionSpec as P


def normalize(stream, gain_vec):
    average = jnp.mean(stream, axis=-1, keepdims=True)
    centred = stream - average
    variance = jnp.mean(centred * centred, axis=-1, keepdims=True)
    return centred * lax.rsqrt(variance + 1e-05) * gain_vec


def encoder(packed, jets, lengths, pair_bins):
    gain_attn, w_qkv, w_out, pair_table, gain_ffn, w_up, w_down, w_phi = packed
    count_jets, slots, width = jets.shape
    heads = pair_table.shape[2]
    head_dim = width // heads
    live_keys = jnp.arange(slots, dtype=jnp.int32)[None, :] < lengths[:, None]
    bin_onehot = (pair_bins[..., None] == jnp.arange(pair_table.shape[1], dtype=jnp.int32)).astype(
        jnp.float32
    )
    stream = jets
    pair_bias = jnp.einsum(
        "jqkb,bh->jhqk", bin_onehot, pair_table[0], precision=lax.Precision.HIGHEST
    )
    normed = (
        normalize(stream.astype(jnp.float32), gain_attn[0])
        .astype(jnp.bfloat16)
        .reshape(count_jets * slots, width)
    )
    projected = jnp.dot(normed, w_qkv[0], preferred_element_type=jnp.float32).astype(jnp.bfloat16)
    projected = projected.reshape(count_jets, slots, 3, heads, head_dim)
    queries = projected[:, :, 0]
    key_rows = projected[:, :, 1]
    value_rows = projected[:, :, 2]
    scores = (
        jnp.einsum("jqhe,jkhe->jhqk", queries, key_rows, preferred_element_type=jnp.float32)
        / math.sqrt(head_dim)
        + pair_bias
    )
    scores = jnp.where(live_keys[:, None, None, :], scores, -1e30)
    attend = jax.nn.softmax(scores, axis=-1).astype(jnp.bfloat16)
    context = jnp.einsum(
        "jhqk,jkhe->jqhe", attend, value_rows, preferred_element_type=jnp.float32
    ).astype(jnp.bfloat16)
    context = context.reshape(count_jets * slots, width)
    middle = stream.astype(jnp.float32).reshape(count_jets * slots, width) + jnp.dot(
        context, w_out[0], preferred_element_type=jnp.float32
    )
    normed = normalize(middle, gain_ffn[0]).astype(jnp.bfloat16)
    hidden = jax.nn.gelu(jnp.dot(normed, w_up[0], preferred_element_type=jnp.float32)).astype(
        jnp.bfloat16
    )
    stream = (middle + jnp.dot(hidden, w_down[0], preferred_element_type=jnp.float32)).astype(
        jnp.bfloat16
    )
    stream = stream.reshape(count_jets, slots, width)
    pooled = jnp.sum(jnp.where(live_keys[..., None], stream.astype(jnp.float32), 0.0), axis=1)
    pooled = (pooled / lengths[:, None].astype(jnp.float32)).astype(jnp.bfloat16)
    return jax.nn.gelu(jnp.dot(pooled, w_phi, preferred_element_type=jnp.float32))


def flow_head(head_weights, summed, number, masses):
    w_mean, w_scale = head_weights
    average = summed / number[..., None]
    centre = jnp.sum(average * w_mean, axis=-1)
    log_width = jnp.sum(average * w_scale, axis=-1)
    return 0.5 * jnp.square((masses - centre) * jnp.exp(-log_width)) + log_width


def butterfly_sum(value, axis, size):
    step = 1
    while step < size:
        pairs = [(index, index ^ step) for index in range(size)]
        value = value + lax.ppermute(value, axis, pairs)
        step *= 2
    return value


def halving_steps(mesh_sizes):
    steps = []
    for axis, size in mesh_sizes:
        step = 1
        while step < size:
            steps.append((axis, step))
            step *= 2
    return steps


def halve_sum(buffer, axis, step, dim=0):
    rows = buffer.shape[dim] // 2
    side = (lax.axis_index(axis) // step) % 2
    keep = lax.dynamic_slice_in_dim(buffer, side * rows, rows, dim)
    send = lax.dynamic_slice_in_dim(buffer, (1 - side) * rows, rows, dim)
    size = lax.axis_size(axis)
    pairs = [(index, index ^ step) for index in range(size)]
    return keep + lax.ppermute(send, axis, pairs)


def double_gather(buffer, axis, step, dim=0):
    rows = buffer.shape[dim]
    side = (lax.axis_index(axis) // step) % 2
    size = lax.axis_size(axis)
    pairs = [(index, index ^ step) for index in range(size)]
    other = lax.ppermute(buffer, axis, pairs)
    shape = list(buffer.shape)
    shape[dim] = 2 * rows
    whole = jnp.zeros(shape, buffer.dtype)
    whole = lax.dynamic_update_slice_in_dim(whole, buffer, side * rows, dim)
    return lax.dynamic_update_slice_in_dim(whole, other, (1 - side) * rows, dim)


def ring_all_reduce(buffer, first, orders, common):
    buffer = halve_sum(buffer, *first)
    colors = jnp.split(buffer, len(orders), axis=0)
    for step_index in range(len(orders[0])):
        colors = [halve_sum(part, *order[step_index]) for part, order in zip(colors, orders)]
    stacked = jnp.stack(colors)
    for axis, step in common:
        size = lax.axis_size(axis)
        pairs = [(index, index ^ step) for index in range(size)]
        stacked = stacked + lax.ppermute(stacked, axis, pairs)
    colors = [stacked[k] for k in range(len(orders))]
    for step_index in reversed(range(len(orders[0]))):
        colors = [double_gather(part, *order[step_index]) for part, order in zip(colors, orders)]
    return double_gather(jnp.concatenate(colors, axis=0), *first)


def shards(
    embed,
    counts,
    member,
    bins,
    masses,
    gain_attn,
    w_qkv,
    w_out,
    pair_table,
    gain_ffn,
    w_up,
    w_down,
    w_phi,
    w_mean,
    w_scale,
):
    packed = (gain_attn, w_qkv, w_out, pair_table, gain_ffn, w_up, w_down, w_phi)
    jets = embed[0]
    lengths = counts[0]
    pair_bins = bins[0]
    group_masses = masses[0]
    groups_total = group_masses.shape[0]
    width = w_phi.shape[1]

    def local_part(params_in):
        return encoder(params_in, jets, lengths, pair_bins)

    phi, back_trunk = jax.vjp(local_part, packed)
    group_onehot = (member[0][:, None] == jnp.arange(groups_total, dtype=jnp.int32)).astype(
        jnp.float32
    )
    partial_sum = jnp.dot(group_onehot.T, phi, precision=lax.Precision.HIGHEST)
    tally = jnp.sum(group_onehot, axis=0)
    stacked = jnp.concatenate(
        [partial_sum, jnp.zeros((1, width), jnp.float32).at[0, :groups_total].set(tally)], axis=0
    )
    stacked = butterfly_sum(stacked, "ens", lax.axis_size("ens"))
    summed = stacked[:groups_total]
    number = stacked[groups_total, :groups_total]

    def head_part(head_weights, summed_in):
        return flow_head(head_weights, summed_in, number, group_masses)

    neg_loglik, back_head = jax.vjp(head_part, (w_mean, w_scale), summed)
    scale_total = 1.0 / (lax.axis_size("dp") * groups_total)
    head_grads, summed_grad = back_head(jnp.full(neg_loglik.shape, scale_total, jnp.float32))
    phi_grad = jnp.dot(group_onehot, summed_grad, precision=lax.Precision.HIGHEST)
    partial_grads = [piece.astype(jnp.float32) for piece in back_trunk(phi_grad)[0]]
    first = (lax.axis_index("ens") == 0).astype(jnp.float32)
    misc = jnp.zeros((8, width), jnp.float32)
    misc = misc.at[0].set(partial_grads[0][0])
    misc = misc.at[1].set(partial_grads[4][0])
    misc = misc.at[2].set(head_grads[0] * first)
    misc = misc.at[3].set(head_grads[1] * first)
    table_size = partial_grads[3].size
    misc = misc.at[4, :table_size].set(partial_grads[3].reshape(-1))
    pieces = [partial_grads[1], partial_grads[2], partial_grads[5], partial_grads[6], partial_grads[7], misc]
    flat = [piece.reshape(-1, width) for piece in pieces]
    offsets = [0]
    for piece in flat:
        offsets.append(offsets[-1] + piece.shape[0])
    steps = halving_steps((("dp", lax.axis_size("dp")), ("ens", lax.axis_size("ens"))))
    first, rest = steps[0], steps[1:]
    near = [("dp", 2), ("ens", 1), ("ens", 4)]
    far = [("ens", 16), ("ens", 2), ("ens", 8)]
    assert sorted(near + far) == sorted(rest)
    count = len(near)
    orders = [near[c:] + near[:c] for c in range(count)]
    quantum = 2 * count << len(near)
    padded = -(-offsets[-1] // quantum) * quantum
    flat.append(jnp.zeros((padded - offsets[-1], width), jnp.float32))
    reduced = ring_all_reduce(jnp.concatenate(flat, axis=0), first, orders, far)
    grad_qkv, grad_out, grad_up, grad_down, grad_phi, misc = [
        reduced[offsets[k] : offsets[k + 1]].reshape(pieces[k].shape) for k in range(len(pieces))
    ]
    return (
        neg_loglik[None, :],
        misc[0][None, :],
        grad_qkv,
        grad_out,
        misc[4, :table_size].reshape(partial_grads[3].shape),
        misc[1][None, :],
        grad_up,
        grad_down,
        grad_phi,
        misc[2],
        misc[3],
    )


def solution(mesh):
    in_specs = (
        P("dp", "ens", None, None),
        P("dp", "ens"),
        P("dp", "ens"),
        P("dp", "ens", None, None),
        P("dp", None),
        P(),
        P(),
        P(),
        P(),
        P(),
        P(),
        P(),
        P(),
        P(),
        P(),
    )
    out_specs = (P("dp", None), P(), P(), P(), P(), P(), P(), P(), P(), P(), P())
    return jax.shard_map(shards, mesh=mesh, in_specs=in_specs, out_specs=out_specs, check_vma=False)
```

```python
import math

import jax
import jax.numpy as jnp
from jax import lax
from jax.sharding import PartitionSpec as P


def normalize(stream, gain_vec):
    average = jnp.mean(stream, axis=-1, keepdims=True)
    centred = stream - average
    variance = jnp.mean(centred * centred, axis=-1, keepdims=True)
    return centred * lax.rsqrt(variance + 1e-05) * gain_vec


def encoder(packed, jets, lengths, pair_bins):
    gain_attn, w_qkv, w_out, pair_table, gain_ffn, w_up, w_down, w_phi = packed
    count_jets, slots, width = jets.shape
    heads = pair_table.shape[2]
    head_dim = width // heads
    live_keys = jnp.arange(slots, dtype=jnp.int32)[None, :] < lengths[:, None]
    bin_onehot = (pair_bins[..., None] == jnp.arange(pair_table.shape[1], dtype=jnp.int32)).astype(
        jnp.float32
    )
    stream = jets
    pair_bias = jnp.einsum(
        "jqkb,bh->jhqk", bin_onehot, pair_table[0], precision=lax.Precision.HIGHEST
    )
    normed = (
        normalize(stream.astype(jnp.float32), gain_attn[0])
        .astype(jnp.bfloat16)
        .reshape(count_jets * slots, width)
    )
    projected = jnp.dot(normed, w_qkv[0], preferred_element_type=jnp.float32).astype(jnp.bfloat16)
    projected = projected.reshape(count_jets, slots, 3, heads, head_dim)
    queries = projected[:, :, 0]
    key_rows = projected[:, :, 1]
    value_rows = projected[:, :, 2]
    scores = (
        jnp.einsum("jqhe,jkhe->jhqk", queries, key_rows, preferred_element_type=jnp.float32)
        / math.sqrt(head_dim)
        + pair_bias
    )
    scores = jnp.where(live_keys[:, None, None, :], scores, -1e30)
    attend = jax.nn.softmax(scores, axis=-1).astype(jnp.bfloat16)
    context = jnp.einsum(
        "jhqk,jkhe->jqhe", attend, value_rows, preferred_element_type=jnp.float32
    ).astype(jnp.bfloat16)
    context = context.reshape(count_jets * slots, width)
    middle = stream.astype(jnp.float32).reshape(count_jets * slots, width) + jnp.dot(
        context, w_out[0], preferred_element_type=jnp.float32
    )
    normed = normalize(middle, gain_ffn[0]).astype(jnp.bfloat16)
    hidden = jax.nn.gelu(jnp.dot(normed, w_up[0], preferred_element_type=jnp.float32)).astype(
        jnp.bfloat16
    )
    stream = (middle + jnp.dot(hidden, w_down[0], preferred_element_type=jnp.float32)).astype(
        jnp.bfloat16
    )
    stream = stream.reshape(count_jets, slots, width)
    pooled = jnp.sum(jnp.where(live_keys[..., None], stream.astype(jnp.float32), 0.0), axis=1)
    pooled = (pooled / lengths[:, None].astype(jnp.float32)).astype(jnp.bfloat16)
    return jax.nn.gelu(jnp.dot(pooled, w_phi, preferred_element_type=jnp.float32))


def flow_head(head_weights, summed, number, masses):
    w_mean, w_scale = head_weights
    average = summed / number[..., None]
    centre = jnp.sum(average * w_mean, axis=-1)
    log_width = jnp.sum(average * w_scale, axis=-1)
    return 0.5 * jnp.square((masses - centre) * jnp.exp(-log_width)) + log_width


def butterfly_sum(value, axis, size):
    step = 1
    while step < size:
        pairs = [(index, index ^ step) for index in range(size)]
        value = value + lax.ppermute(value, axis, pairs)
        step *= 2
    return value


def halving_steps(mesh_sizes):
    steps = []
    for axis, size in mesh_sizes:
        step = 1
        while step < size:
            steps.append((axis, step))
            step *= 2
    return steps


def halve_sum(buffer, axis, step, dim=0):
    rows = buffer.shape[dim] // 2
    side = (lax.axis_index(axis) // step) % 2
    keep = lax.dynamic_slice_in_dim(buffer, side * rows, rows, dim)
    send = lax.dynamic_slice_in_dim(buffer, (1 - side) * rows, rows, dim)
    size = lax.axis_size(axis)
    pairs = [(index, index ^ step) for index in range(size)]
    return keep + lax.ppermute(send, axis, pairs)


def double_gather(buffer, axis, step, dim=0):
    rows = buffer.shape[dim]
    side = (lax.axis_index(axis) // step) % 2
    size = lax.axis_size(axis)
    pairs = [(index, index ^ step) for index in range(size)]
    other = lax.ppermute(buffer, axis, pairs)
    shape = list(buffer.shape)
    shape[dim] = 2 * rows
    whole = jnp.zeros(shape, buffer.dtype)
    whole = lax.dynamic_update_slice_in_dim(whole, buffer, side * rows, dim)
    return lax.dynamic_update_slice_in_dim(whole, other, (1 - side) * rows, dim)


def ring_all_reduce(buffer, first, orders, common):
    buffer = halve_sum(buffer, *first)
    colors = jnp.split(buffer, len(orders), axis=0)
    for step_index in range(len(orders[0])):
        colors = [halve_sum(part, *order[step_index]) for part, order in zip(colors, orders)]
    stacked = jnp.stack(colors)
    for axis, step in common:
        size = lax.axis_size(axis)
        pairs = [(index, index ^ step) for index in range(size)]
        stacked = stacked + lax.ppermute(stacked, axis, pairs)
    colors = [stacked[k] for k in range(len(orders))]
    for step_index in reversed(range(len(orders[0]))):
        colors = [double_gather(part, *order[step_index]) for part, order in zip(colors, orders)]
    return double_gather(jnp.concatenate(colors, axis=0), *first)


def shards(
    embed,
    counts,
    member,
    bins,
    masses,
    gain_attn,
    w_qkv,
    w_out,
    pair_table,
    gain_ffn,
    w_up,
    w_down,
    w_phi,
    w_mean,
    w_scale,
):
    packed = (gain_attn, w_qkv, w_out, pair_table, gain_ffn, w_up, w_down, w_phi)
    jets = embed[0]
    lengths = counts[0]
    pair_bins = bins[0]
    group_masses = masses[0]
    groups_total = group_masses.shape[0]
    width = w_phi.shape[1]

    def local_part(params_in):
        return encoder(params_in, jets, lengths, pair_bins)

    phi, back_trunk = jax.vjp(local_part, packed)
    group_onehot = (member[0][:, None] == jnp.arange(groups_total, dtype=jnp.int32)).astype(
        jnp.float32
    )
    partial_sum = jnp.dot(group_onehot.T, phi, precision=lax.Precision.HIGHEST)
    tally = jnp.sum(group_onehot, axis=0)
    stacked = jnp.concatenate(
        [partial_sum, jnp.zeros((1, width), jnp.float32).at[0, :groups_total].set(tally)], axis=0
    )
    stacked = butterfly_sum(stacked, "ens", lax.axis_size("ens"))
    summed = stacked[:groups_total]
    number = stacked[groups_total, :groups_total]

    def head_part(head_weights, summed_in):
        return flow_head(head_weights, summed_in, number, group_masses)

    neg_loglik, back_head = jax.vjp(head_part, (w_mean, w_scale), summed)
    scale_total = 1.0 / (lax.axis_size("dp") * groups_total)
    head_grads, summed_grad = back_head(jnp.full(neg_loglik.shape, scale_total, jnp.float32))
    phi_grad = jnp.dot(group_onehot, summed_grad, precision=lax.Precision.HIGHEST)
    partial_grads = [piece.astype(jnp.float32) for piece in back_trunk(phi_grad)[0]]
    first = (lax.axis_index("ens") == 0).astype(jnp.float32)
    misc = jnp.zeros((8, width), jnp.float32)
    misc = misc.at[0].set(partial_grads[0][0])
    misc = misc.at[1].set(partial_grads[4][0])
    misc = misc.at[2].set(head_grads[0] * first)
    misc = misc.at[3].set(head_grads[1] * first)
    table_size = partial_grads[3].size
    misc = misc.at[4, :table_size].set(partial_grads[3].reshape(-1))
    pieces = [partial_grads[1], partial_grads[2], partial_grads[5], partial_grads[6], partial_grads[7], misc]
    flat = [
        block
        for piece in pieces
        for block in jnp.split(piece.reshape(-1, piece.shape[-1]), piece.shape[-1] // width, axis=1)
    ]
    offsets = [0]
    for piece in flat:
        offsets.append(offsets[-1] + piece.shape[0])
    steps = halving_steps((("dp", lax.axis_size("dp")), ("ens", lax.axis_size("ens"))))
    first, rest = steps[0], steps[1:]
    near = [("dp", 2), ("ens", 1), ("ens", 4)]
    far = [("ens", 16), ("ens", 2), ("ens", 8)]
    assert sorted(near + far) == sorted(rest)
    count = len(near)
    orders = [near[c:] + near[:c] for c in range(count)]
    quantum = 2 * count << len(near)
    padded = -(-offsets[-1] // quantum) * quantum
    flat.append(jnp.zeros((padded - offsets[-1], width), jnp.float32))
    reduced = ring_all_reduce(jnp.concatenate(flat, axis=0), first, orders, far)
    blocks = [reduced[offsets[k] : offsets[k + 1]] for k in range(len(flat) - 1)]
    unpacked = []
    for piece in pieces:
        parts = piece.shape[-1] // width
        unpacked.append(jnp.concatenate(blocks[:parts], axis=1).reshape(piece.shape))
        blocks = blocks[parts:]
    grad_qkv, grad_out, grad_up, grad_down, grad_phi, misc = unpacked
    return (
        neg_loglik[None, :],
        misc[0][None, :],
        grad_qkv,
        grad_out,
        misc[4, :table_size].reshape(partial_grads[3].shape),
        misc[1][None, :],
        grad_up,
        grad_down,
        grad_phi,
        misc[2],
        misc[3],
    )


def solution(mesh):
    in_specs = (
        P("dp", "ens", None, None),
        P("dp", "ens"),
        P("dp", "ens"),
        P("dp", "ens", None, None),
        P("dp", None),
        P(),
        P(),
        P(),
        P(),
        P(),
        P(),
        P(),
        P(),
        P(),
        P(),
    )
    out_specs = (P("dp", None), P(), P(), P(), P(), P(), P(), P(), P(), P(), P())
    return jax.shard_map(shards, mesh=mesh, in_specs=in_specs, out_specs=out_specs, check_vma=False)
```

```python
import math

import jax
import jax.numpy as jnp
from jax import lax
from jax.sharding import PartitionSpec as P


def normalize(stream, gain_vec):
    average = jnp.mean(stream, axis=-1, keepdims=True)
    centred = stream - average
    variance = jnp.mean(centred * centred, axis=-1, keepdims=True)
    return centred * lax.rsqrt(variance + 1e-05) * gain_vec


def lookup_value(table, pair_bins):
    heads = table.shape[1]
    shape = (pair_bins.shape[0], heads) + pair_bins.shape[1:]
    levels = pair_bins[:, None, :, :]
    bias = jnp.broadcast_to(table[0][None, :, None, None], shape)
    for level in range(1, table.shape[0]):
        bias = jnp.where(levels == level, table[level][None, :, None, None], bias)
    return bias


@jax.custom_vjp
def bias_lookup(table, pair_bins):
    return lookup_value(table, pair_bins)


def bias_lookup_fwd(table, pair_bins):
    return lookup_value(table, pair_bins), (pair_bins, table)


def bias_lookup_bwd(residuals, grad):
    pair_bins, table = residuals
    levels = jnp.arange(table.shape[0], dtype=jnp.int32)
    onehot = (pair_bins[..., None] == levels).astype(jnp.float32)
    table_grad = jnp.einsum("jqkb,jhqk->bh", onehot, grad, precision=lax.Precision.HIGHEST)
    return table_grad, None


bias_lookup.defvjp(bias_lookup_fwd, bias_lookup_bwd)


def encoder(packed, jets, lengths, pair_bins):
    gain_attn, w_qkv, w_out, pair_table, gain_ffn, w_up, w_down, w_phi = packed
    count_jets, slots, width = jets.shape
    heads = pair_table.shape[2]
    head_dim = width // heads
    live_keys = jnp.arange(slots, dtype=jnp.int32)[None, :] < lengths[:, None]
    stream = jets
    pair_bias = bias_lookup(pair_table[0], pair_bins)
    normed = (
        normalize(stream.astype(jnp.float32), gain_attn[0])
        .astype(jnp.bfloat16)
        .reshape(count_jets * slots, width)
    )
    projected = jnp.dot(normed, w_qkv[0], preferred_element_type=jnp.float32).astype(jnp.bfloat16)
    projected = projected.reshape(count_jets, slots, 3, heads, head_dim)
    queries = projected[:, :, 0]
    key_rows = projected[:, :, 1]
    value_rows = projected[:, :, 2]
    scores = (
        jnp.einsum("jqhe,jkhe->jhqk", queries, key_rows, preferred_element_type=jnp.float32)
        / math.sqrt(head_dim)
        + pair_bias
    )
    scores = jnp.where(live_keys[:, None, None, :], scores, -1e30)
    attend = jax.nn.softmax(scores, axis=-1).astype(jnp.bfloat16)
    context = jnp.einsum(
        "jhqk,jkhe->jqhe", attend, value_rows, preferred_element_type=jnp.float32
    ).astype(jnp.bfloat16)
    context = context.reshape(count_jets * slots, width)
    middle = stream.astype(jnp.float32).reshape(count_jets * slots, width) + jnp.dot(
        context, w_out[0], preferred_element_type=jnp.float32
    )
    normed = normalize(middle, gain_ffn[0]).astype(jnp.bfloat16)
    hidden = jax.nn.gelu(jnp.dot(normed, w_up[0], preferred_element_type=jnp.float32)).astype(
        jnp.bfloat16
    )
    stream = (middle + jnp.dot(hidden, w_down[0], preferred_element_type=jnp.float32)).astype(
        jnp.bfloat16
    )
    stream = stream.reshape(count_jets, slots, width)
    pooled = jnp.sum(jnp.where(live_keys[..., None], stream.astype(jnp.float32), 0.0), axis=1)
    pooled = (pooled / lengths[:, None].astype(jnp.float32)).astype(jnp.bfloat16)
    return jax.nn.gelu(jnp.dot(pooled, w_phi, preferred_element_type=jnp.float32))


def flow_head(head_weights, summed, number, masses):
    w_mean, w_scale = head_weights
    average = summed / number[..., None]
    centre = jnp.sum(average * w_mean, axis=-1)
    log_width = jnp.sum(average * w_scale, axis=-1)
    return 0.5 * jnp.square((masses - centre) * jnp.exp(-log_width)) + log_width


def butterfly_sum(value, axis, size):
    step = 1
    while step < size:
        pairs = [(index, index ^ step) for index in range(size)]
        value = value + lax.ppermute(value, axis, pairs)
        step *= 2
    return value


def halving_steps(mesh_sizes):
    steps = []
    for axis, size in mesh_sizes:
        step = 1
        while step < size:
            steps.append((axis, step))
            step *= 2
    return steps


def halve_sum(buffer, axis, step, dim=0):
    rows = buffer.shape[dim] // 2
    side = (lax.axis_index(axis) // step) % 2
    keep = lax.dynamic_slice_in_dim(buffer, side * rows, rows, dim)
    send = lax.dynamic_slice_in_dim(buffer, (1 - side) * rows, rows, dim)
    size = lax.axis_size(axis)
    pairs = [(index, index ^ step) for index in range(size)]
    return keep + lax.ppermute(send, axis, pairs)


def double_gather(buffer, axis, step, dim=0):
    rows = buffer.shape[dim]
    side = (lax.axis_index(axis) // step) % 2
    size = lax.axis_size(axis)
    pairs = [(index, index ^ step) for index in range(size)]
    other = lax.ppermute(buffer, axis, pairs)
    shape = list(buffer.shape)
    shape[dim] = 2 * rows
    whole = jnp.zeros(shape, buffer.dtype)
    whole = lax.dynamic_update_slice_in_dim(whole, buffer, side * rows, dim)
    return lax.dynamic_update_slice_in_dim(whole, other, (1 - side) * rows, dim)


def ring_all_reduce(buffer, first, orders, common):
    buffer = halve_sum(buffer, *first)
    colors = jnp.split(buffer, len(orders), axis=0)
    for step_index in range(len(orders[0])):
        colors = [halve_sum(part, *order[step_index]) for part, order in zip(colors, orders)]
    stacked = jnp.stack(colors)
    for axis, step in common:
        size = lax.axis_size(axis)
        pairs = [(index, index ^ step) for index in range(size)]
        stacked = stacked + lax.ppermute(stacked, axis, pairs)
    colors = [stacked[k] for k in range(len(orders))]
    for step_index in reversed(range(len(orders[0]))):
        colors = [double_gather(part, *order[step_index]) for part, order in zip(colors, orders)]
    return double_gather(jnp.concatenate(colors, axis=0), *first)


def shards(
    embed,
    counts,
    member,
    bins,
    masses,
    gain_attn,
    w_qkv,
    w_out,
    pair_table,
    gain_ffn,
    w_up,
    w_down,
    w_phi,
    w_mean,
    w_scale,
):
    packed = (gain_attn, w_qkv, w_out, pair_table, gain_ffn, w_up, w_down, w_phi)
    jets = embed[0]
    lengths = counts[0]
    pair_bins = bins[0]
    group_masses = masses[0]
    groups_total = group_masses.shape[0]
    width = w_phi.shape[1]

    def local_part(params_in):
        return encoder(params_in, jets, lengths, pair_bins)

    phi, back_trunk = jax.vjp(local_part, packed)
    group_onehot = (member[0][:, None] == jnp.arange(groups_total, dtype=jnp.int32)).astype(
        jnp.float32
    )
    partial_sum = jnp.dot(group_onehot.T, phi, precision=lax.Precision.HIGHEST)
    tally = jnp.sum(group_onehot, axis=0)
    stacked = jnp.concatenate(
        [partial_sum, jnp.zeros((1, width), jnp.float32).at[0, :groups_total].set(tally)], axis=0
    )
    stacked = butterfly_sum(stacked, "ens", lax.axis_size("ens"))
    summed = stacked[:groups_total]
    number = stacked[groups_total, :groups_total]

    def head_part(head_weights, summed_in):
        return flow_head(head_weights, summed_in, number, group_masses)

    neg_loglik, back_head = jax.vjp(head_part, (w_mean, w_scale), summed)
    scale_total = 1.0 / (lax.axis_size("dp") * groups_total)
    head_grads, summed_grad = back_head(jnp.full(neg_loglik.shape, scale_total, jnp.float32))
    phi_grad = jnp.dot(group_onehot, summed_grad, precision=lax.Precision.HIGHEST)
    partial_grads = [piece.astype(jnp.float32) for piece in back_trunk(phi_grad)[0]]
    first = (lax.axis_index("ens") == 0).astype(jnp.float32)
    misc = jnp.zeros((8, width), jnp.float32)
    misc = misc.at[0].set(partial_grads[0][0])
    misc = misc.at[1].set(partial_grads[4][0])
    misc = misc.at[2].set(head_grads[0] * first)
    misc = misc.at[3].set(head_grads[1] * first)
    table_size = partial_grads[3].size
    misc = misc.at[4, :table_size].set(partial_grads[3].reshape(-1))
    pieces = [partial_grads[1], partial_grads[2], partial_grads[5], partial_grads[6], partial_grads[7], misc]
    flat = [piece.reshape(-1, width) for piece in pieces]
    offsets = [0]
    for piece in flat:
        offsets.append(offsets[-1] + piece.shape[0])
    steps = halving_steps((("dp", lax.axis_size("dp")), ("ens", lax.axis_size("ens"))))
    first, rest = steps[0], steps[1:]
    near = [("dp", 2), ("ens", 1), ("ens", 4)]
    far = [("ens", 16), ("ens", 2), ("ens", 8)]
    assert sorted(near + far) == sorted(rest)
    count = len(near)
    orders = [near[c:] + near[:c] for c in range(count)]
    quantum = 2 * count << len(near)
    padded = -(-offsets[-1] // quantum) * quantum
    flat.append(jnp.zeros((padded - offsets[-1], width), jnp.float32))
    reduced = ring_all_reduce(jnp.concatenate(flat, axis=0), first, orders, far)
    grad_qkv, grad_out, grad_up, grad_down, grad_phi, misc = [
        reduced[offsets[k] : offsets[k + 1]].reshape(pieces[k].shape) for k in range(len(pieces))
    ]
    return (
        neg_loglik[None, :],
        misc[0][None, :],
        grad_qkv,
        grad_out,
        misc[4, :table_size].reshape(partial_grads[3].shape),
        misc[1][None, :],
        grad_up,
        grad_down,
        grad_phi,
        misc[2],
        misc[3],
    )


def solution(mesh):
    in_specs = (
        P("dp", "ens", None, None),
        P("dp", "ens"),
        P("dp", "ens"),
        P("dp", "ens", None, None),
        P("dp", None),
        P(),
        P(),
        P(),
        P(),
        P(),
        P(),
        P(),
        P(),
        P(),
        P(),
    )
    out_specs = (P("dp", None), P(), P(), P(), P(), P(), P(), P(), P(), P(), P())
    return jax.shard_map(shards, mesh=mesh, in_specs=in_specs, out_specs=out_specs, check_vma=False)
```

```python
import math

import jax
import jax.numpy as jnp
from jax import lax
from jax.sharding import PartitionSpec as P


def normalize(stream, gain_vec):
    average = jnp.mean(stream, axis=-1, keepdims=True)
    centred = stream - average
    variance = jnp.mean(centred * centred, axis=-1, keepdims=True)
    return centred * lax.rsqrt(variance + 1e-05) * gain_vec


def lookup_value(table, pair_bins):
    heads = table.shape[1]
    shape = (pair_bins.shape[0], heads) + pair_bins.shape[1:]
    levels = pair_bins[:, None, :, :]
    values = [table[level][None, :, None, None] for level in range(table.shape[0])]
    bit = 0
    while len(values) > 1:
        if len(values) % 2:
            values.append(values[-1])
        chosen = (levels >> bit) % 2 == 1
        values = [jnp.where(chosen, values[k + 1], values[k]) for k in range(0, len(values), 2)]
        bit += 1
    return jnp.broadcast_to(values[0], shape)


@jax.custom_vjp
def bias_lookup(table, pair_bins):
    return lookup_value(table, pair_bins)


def bias_lookup_fwd(table, pair_bins):
    return lookup_value(table, pair_bins), (pair_bins, table)


def bias_lookup_bwd(residuals, grad):
    pair_bins, table = residuals
    levels = jnp.arange(table.shape[0], dtype=jnp.int32)
    onehot = (pair_bins[..., None] == levels).astype(jnp.float32)
    table_grad = jnp.einsum("jqkb,jhqk->bh", onehot, grad, precision=lax.Precision.HIGHEST)
    return table_grad, None


bias_lookup.defvjp(bias_lookup_fwd, bias_lookup_bwd)


def encoder(packed, jets, lengths, pair_bins):
    gain_attn, w_qkv, w_out, pair_table, gain_ffn, w_up, w_down, w_phi = packed
    count_jets, slots, width = jets.shape
    heads = pair_table.shape[2]
    head_dim = width // heads
    live_keys = jnp.arange(slots, dtype=jnp.int32)[None, :] < lengths[:, None]
    stream = jets
    pair_bias = bias_lookup(pair_table[0], pair_bins)
    normed = (
        normalize(stream.astype(jnp.float32), gain_attn[0])
        .astype(jnp.bfloat16)
        .reshape(count_jets * slots, width)
    )
    projected = jnp.dot(normed, w_qkv[0], preferred_element_type=jnp.float32).astype(jnp.bfloat16)
    projected = projected.reshape(count_jets, slots, 3, heads, head_dim)
    queries = projected[:, :, 0]
    key_rows = projected[:, :, 1]
    value_rows = projected[:, :, 2]
    scores = (
        jnp.einsum("jqhe,jkhe->jhqk", queries, key_rows, preferred_element_type=jnp.float32)
        / math.sqrt(head_dim)
        + pair_bias
    )
    scores = jnp.where(live_keys[:, None, None, :], scores, -1e30)
    attend = jax.nn.softmax(scores, axis=-1).astype(jnp.bfloat16)
    context = jnp.einsum(
        "jhqk,jkhe->jqhe", attend, value_rows, preferred_element_type=jnp.float32
    ).astype(jnp.bfloat16)
    context = context.reshape(count_jets * slots, width)
    middle = stream.astype(jnp.float32).reshape(count_jets * slots, width) + jnp.dot(
        context, w_out[0], preferred_element_type=jnp.float32
    )
    normed = normalize(middle, gain_ffn[0]).astype(jnp.bfloat16)
    hidden = jax.nn.gelu(jnp.dot(normed, w_up[0], preferred_element_type=jnp.float32)).astype(
        jnp.bfloat16
    )
    stream = (middle + jnp.dot(hidden, w_down[0], preferred_element_type=jnp.float32)).astype(
        jnp.bfloat16
    )
    stream = stream.reshape(count_jets, slots, width)
    pooled = jnp.sum(jnp.where(live_keys[..., None], stream.astype(jnp.float32), 0.0), axis=1)
    pooled = (pooled / lengths[:, None].astype(jnp.float32)).astype(jnp.bfloat16)
    return jax.nn.gelu(jnp.dot(pooled, w_phi, preferred_element_type=jnp.float32))


def flow_head(head_weights, summed, number, masses):
    w_mean, w_scale = head_weights
    average = summed / number[..., None]
    centre = jnp.sum(average * w_mean, axis=-1)
    log_width = jnp.sum(average * w_scale, axis=-1)
    return 0.5 * jnp.square((masses - centre) * jnp.exp(-log_width)) + log_width


def butterfly_sum(value, axis, size):
    step = 1
    while step < size:
        pairs = [(index, index ^ step) for index in range(size)]
        value = value + lax.ppermute(value, axis, pairs)
        step *= 2
    return value


def halving_steps(mesh_sizes):
    steps = []
    for axis, size in mesh_sizes:
        step = 1
        while step < size:
            steps.append((axis, step))
            step *= 2
    return steps


def halve_sum(buffer, axis, step, dim=0):
    rows = buffer.shape[dim] // 2
    side = (lax.axis_index(axis) // step) % 2
    keep = lax.dynamic_slice_in_dim(buffer, side * rows, rows, dim)
    send = lax.dynamic_slice_in_dim(buffer, (1 - side) * rows, rows, dim)
    size = lax.axis_size(axis)
    pairs = [(index, index ^ step) for index in range(size)]
    return keep + lax.ppermute(send, axis, pairs)


def double_gather(buffer, axis, step, dim=0):
    rows = buffer.shape[dim]
    side = (lax.axis_index(axis) // step) % 2
    size = lax.axis_size(axis)
    pairs = [(index, index ^ step) for index in range(size)]
    other = lax.ppermute(buffer, axis, pairs)
    shape = list(buffer.shape)
    shape[dim] = 2 * rows
    whole = jnp.zeros(shape, buffer.dtype)
    whole = lax.dynamic_update_slice_in_dim(whole, buffer, side * rows, dim)
    return lax.dynamic_update_slice_in_dim(whole, other, (1 - side) * rows, dim)


def ring_all_reduce(buffer, first, orders, common):
    buffer = halve_sum(buffer, *first)
    colors = jnp.split(buffer, len(orders), axis=0)
    for step_index in range(len(orders[0])):
        colors = [halve_sum(part, *order[step_index]) for part, order in zip(colors, orders)]
    stacked = jnp.stack(colors)
    for axis, step in common:
        size = lax.axis_size(axis)
        pairs = [(index, index ^ step) for index in range(size)]
        stacked = stacked + lax.ppermute(stacked, axis, pairs)
    colors = [stacked[k] for k in range(len(orders))]
    for step_index in reversed(range(len(orders[0]))):
        colors = [double_gather(part, *order[step_index]) for part, order in zip(colors, orders)]
    return double_gather(jnp.concatenate(colors, axis=0), *first)


def shards(
    embed,
    counts,
    member,
    bins,
    masses,
    gain_attn,
    w_qkv,
    w_out,
    pair_table,
    gain_ffn,
    w_up,
    w_down,
    w_phi,
    w_mean,
    w_scale,
):
    packed = (gain_attn, w_qkv, w_out, pair_table, gain_ffn, w_up, w_down, w_phi)
    jets = embed[0]
    lengths = counts[0]
    pair_bins = bins[0]
    group_masses = masses[0]
    groups_total = group_masses.shape[0]
    width = w_phi.shape[1]

    def local_part(params_in):
        return encoder(params_in, jets, lengths, pair_bins)

    phi, back_trunk = jax.vjp(local_part, packed)
    group_onehot = (member[0][:, None] == jnp.arange(groups_total, dtype=jnp.int32)).astype(
        jnp.float32
    )
    partial_sum = jnp.dot(group_onehot.T, phi, precision=lax.Precision.HIGHEST)
    tally = jnp.sum(group_onehot, axis=0)
    stacked = jnp.concatenate(
        [partial_sum, jnp.zeros((1, width), jnp.float32).at[0, :groups_total].set(tally)], axis=0
    )
    stacked = butterfly_sum(stacked, "ens", lax.axis_size("ens"))
    summed = stacked[:groups_total]
    number = stacked[groups_total, :groups_total]

    def head_part(head_weights, summed_in):
        return flow_head(head_weights, summed_in, number, group_masses)

    neg_loglik, back_head = jax.vjp(head_part, (w_mean, w_scale), summed)
    scale_total = 1.0 / (lax.axis_size("dp") * groups_total)
    head_grads, summed_grad = back_head(jnp.full(neg_loglik.shape, scale_total, jnp.float32))
    phi_grad = jnp.dot(group_onehot, summed_grad, precision=lax.Precision.HIGHEST)
    partial_grads = [piece.astype(jnp.float32) for piece in back_trunk(phi_grad)[0]]
    first = (lax.axis_index("ens") == 0).astype(jnp.float32)
    misc = jnp.zeros((8, width), jnp.float32)
    misc = misc.at[0].set(partial_grads[0][0])
    misc = misc.at[1].set(partial_grads[4][0])
    misc = misc.at[2].set(head_grads[0] * first)
    misc = misc.at[3].set(head_grads[1] * first)
    table_size = partial_grads[3].size
    misc = misc.at[4, :table_size].set(partial_grads[3].reshape(-1))
    pieces = [partial_grads[1], partial_grads[2], partial_grads[5], partial_grads[6], partial_grads[7], misc]
    flat = [piece.reshape(-1, width) for piece in pieces]
    offsets = [0]
    for piece in flat:
        offsets.append(offsets[-1] + piece.shape[0])
    steps = halving_steps((("dp", lax.axis_size("dp")), ("ens", lax.axis_size("ens"))))
    first, rest = steps[0], steps[1:]
    near = [("dp", 2), ("ens", 1), ("ens", 4)]
    far = [("ens", 16), ("ens", 2), ("ens", 8)]
    assert sorted(near + far) == sorted(rest)
    count = len(near)
    orders = [near[c:] + near[:c] for c in range(count)]
    quantum = 2 * count << len(near)
    padded = -(-offsets[-1] // quantum) * quantum
    flat.append(jnp.zeros((padded - offsets[-1], width), jnp.float32))
    reduced = ring_all_reduce(jnp.concatenate(flat, axis=0), first, orders, far)
    grad_qkv, grad_out, grad_up, grad_down, grad_phi, misc = [
        reduced[offsets[k] : offsets[k + 1]].reshape(pieces[k].shape) for k in range(len(pieces))
    ]
    return (
        neg_loglik[None, :],
        misc[0][None, :],
        grad_qkv,
        grad_out,
        misc[4, :table_size].reshape(partial_grads[3].shape),
        misc[1][None, :],
        grad_up,
        grad_down,
        grad_phi,
        misc[2],
        misc[3],
    )


def solution(mesh):
    in_specs = (
        P("dp", "ens", None, None),
        P("dp", "ens"),
        P("dp", "ens"),
        P("dp", "ens", None, None),
        P("dp", None),
        P(),
        P(),
        P(),
        P(),
        P(),
        P(),
        P(),
        P(),
        P(),
        P(),
    )
    out_specs = (P("dp", None), P(), P(), P(), P(), P(), P(), P(), P(), P(), P())
    return jax.shard_map(shards, mesh=mesh, in_specs=in_specs, out_specs=out_specs, check_vma=False)
```

```python
import math

import jax
import jax.numpy as jnp
from jax import lax
from jax.sharding import PartitionSpec as P


def normalize(stream, gain_vec):
    average = jnp.mean(stream, axis=-1, keepdims=True)
    centred = stream - average
    variance = jnp.mean(centred * centred, axis=-1, keepdims=True)
    return centred * lax.rsqrt(variance + 1e-05) * gain_vec


def lookup_value(table, pair_bins):
    heads = table.shape[1]
    shape = (pair_bins.shape[0], heads) + pair_bins.shape[1:]
    levels = pair_bins[:, None, :, :]
    values = [table[level][None, :, None, None] for level in range(table.shape[0])]
    bit = 0
    while len(values) > 1:
        if len(values) % 2:
            values.append(values[-1])
        chosen = (levels >> bit) % 2 == 1
        values = [jnp.where(chosen, values[k + 1], values[k]) for k in range(0, len(values), 2)]
        bit += 1
    return jnp.broadcast_to(values[0], shape)


@jax.custom_vjp
def bias_lookup(table, pair_bins):
    return lookup_value(table, pair_bins)


def bias_lookup_fwd(table, pair_bins):
    return lookup_value(table, pair_bins), (pair_bins, table)


def bias_lookup_bwd(residuals, grad):
    pair_bins, table = residuals
    levels = pair_bins[:, None, :, :]
    table_grad = jnp.stack(
        [
            jnp.sum(jnp.where(levels == level, grad, 0.0), axis=(0, 2, 3))
            for level in range(table.shape[0])
        ]
    )
    return table_grad, None


bias_lookup.defvjp(bias_lookup_fwd, bias_lookup_bwd)


def encoder(packed, jets, lengths, pair_bins):
    gain_attn, w_qkv, w_out, pair_table, gain_ffn, w_up, w_down, w_phi = packed
    count_jets, slots, width = jets.shape
    heads = pair_table.shape[2]
    head_dim = width // heads
    live_keys = jnp.arange(slots, dtype=jnp.int32)[None, :] < lengths[:, None]
    stream = jets
    pair_bias = bias_lookup(pair_table[0], pair_bins)
    normed = (
        normalize(stream.astype(jnp.float32), gain_attn[0])
        .astype(jnp.bfloat16)
        .reshape(count_jets * slots, width)
    )
    projected = jnp.dot(normed, w_qkv[0], preferred_element_type=jnp.float32).astype(jnp.bfloat16)
    projected = projected.reshape(count_jets, slots, 3, heads, head_dim)
    queries = projected[:, :, 0]
    key_rows = projected[:, :, 1]
    value_rows = projected[:, :, 2]
    scores = (
        jnp.einsum("jqhe,jkhe->jhqk", queries, key_rows, preferred_element_type=jnp.float32)
        / math.sqrt(head_dim)
        + pair_bias
    )
    scores = jnp.where(live_keys[:, None, None, :], scores, -1e30)
    attend = jax.nn.softmax(scores, axis=-1).astype(jnp.bfloat16)
    context = jnp.einsum(
        "jhqk,jkhe->jqhe", attend, value_rows, preferred_element_type=jnp.float32
    ).astype(jnp.bfloat16)
    context = context.reshape(count_jets * slots, width)
    middle = stream.astype(jnp.float32).reshape(count_jets * slots, width) + jnp.dot(
        context, w_out[0], preferred_element_type=jnp.float32
    )
    normed = normalize(middle, gain_ffn[0]).astype(jnp.bfloat16)
    hidden = jax.nn.gelu(jnp.dot(normed, w_up[0], preferred_element_type=jnp.float32)).astype(
        jnp.bfloat16
    )
    stream = (middle + jnp.dot(hidden, w_down[0], preferred_element_type=jnp.float32)).astype(
        jnp.bfloat16
    )
    stream = stream.reshape(count_jets, slots, width)
    pooled = jnp.sum(jnp.where(live_keys[..., None], stream.astype(jnp.float32), 0.0), axis=1)
    pooled = (pooled / lengths[:, None].astype(jnp.float32)).astype(jnp.bfloat16)
    return jax.nn.gelu(jnp.dot(pooled, w_phi, preferred_element_type=jnp.float32))


def flow_head(head_weights, summed, number, masses):
    w_mean, w_scale = head_weights
    average = summed / number[..., None]
    centre = jnp.sum(average * w_mean, axis=-1)
    log_width = jnp.sum(average * w_scale, axis=-1)
    return 0.5 * jnp.square((masses - centre) * jnp.exp(-log_width)) + log_width


def butterfly_sum(value, axis, size):
    step = 1
    while step < size:
        pairs = [(index, index ^ step) for index in range(size)]
        value = value + lax.ppermute(value, axis, pairs)
        step *= 2
    return value


def halving_steps(mesh_sizes):
    steps = []
    for axis, size in mesh_sizes:
        step = 1
        while step < size:
            steps.append((axis, step))
            step *= 2
    return steps


def halve_sum(buffer, axis, step, dim=0):
    rows = buffer.shape[dim] // 2
    side = (lax.axis_index(axis) // step) % 2
    keep = lax.dynamic_slice_in_dim(buffer, side * rows, rows, dim)
    send = lax.dynamic_slice_in_dim(buffer, (1 - side) * rows, rows, dim)
    size = lax.axis_size(axis)
    pairs = [(index, index ^ step) for index in range(size)]
    return keep + lax.ppermute(send, axis, pairs)


def double_gather(buffer, axis, step, dim=0):
    rows = buffer.shape[dim]
    side = (lax.axis_index(axis) // step) % 2
    size = lax.axis_size(axis)
    pairs = [(index, index ^ step) for index in range(size)]
    other = lax.ppermute(buffer, axis, pairs)
    shape = list(buffer.shape)
    shape[dim] = 2 * rows
    whole = jnp.zeros(shape, buffer.dtype)
    whole = lax.dynamic_update_slice_in_dim(whole, buffer, side * rows, dim)
    return lax.dynamic_update_slice_in_dim(whole, other, (1 - side) * rows, dim)


def ring_all_reduce(buffer, first, orders, common):
    buffer = halve_sum(buffer, *first)
    colors = jnp.split(buffer, len(orders), axis=0)
    for step_index in range(len(orders[0])):
        colors = [halve_sum(part, *order[step_index]) for part, order in zip(colors, orders)]
    stacked = jnp.stack(colors)
    for axis, step in common:
        size = lax.axis_size(axis)
        pairs = [(index, index ^ step) for index in range(size)]
        stacked = stacked + lax.ppermute(stacked, axis, pairs)
    colors = [stacked[k] for k in range(len(orders))]
    for step_index in reversed(range(len(orders[0]))):
        colors = [double_gather(part, *order[step_index]) for part, order in zip(colors, orders)]
    return double_gather(jnp.concatenate(colors, axis=0), *first)


def shards(
    embed,
    counts,
    member,
    bins,
    masses,
    gain_attn,
    w_qkv,
    w_out,
    pair_table,
    gain_ffn,
    w_up,
    w_down,
    w_phi,
    w_mean,
    w_scale,
):
    packed = (gain_attn, w_qkv, w_out, pair_table, gain_ffn, w_up, w_down, w_phi)
    jets = embed[0]
    lengths = counts[0]
    pair_bins = bins[0]
    group_masses = masses[0]
    groups_total = group_masses.shape[0]
    width = w_phi.shape[1]

    def local_part(params_in):
        return encoder(params_in, jets, lengths, pair_bins)

    phi, back_trunk = jax.vjp(local_part, packed)
    group_onehot = (member[0][:, None] == jnp.arange(groups_total, dtype=jnp.int32)).astype(
        jnp.float32
    )
    partial_sum = jnp.dot(group_onehot.T, phi, precision=lax.Precision.HIGHEST)
    tally = jnp.sum(group_onehot, axis=0)
    stacked = jnp.concatenate(
        [partial_sum, jnp.zeros((1, width), jnp.float32).at[0, :groups_total].set(tally)], axis=0
    )
    stacked = butterfly_sum(stacked, "ens", lax.axis_size("ens"))
    summed = stacked[:groups_total]
    number = stacked[groups_total, :groups_total]

    def head_part(head_weights, summed_in):
        return flow_head(head_weights, summed_in, number, group_masses)

    neg_loglik, back_head = jax.vjp(head_part, (w_mean, w_scale), summed)
    scale_total = 1.0 / (lax.axis_size("dp") * groups_total)
    head_grads, summed_grad = back_head(jnp.full(neg_loglik.shape, scale_total, jnp.float32))
    phi_grad = jnp.dot(group_onehot, summed_grad, precision=lax.Precision.HIGHEST)
    partial_grads = [piece.astype(jnp.float32) for piece in back_trunk(phi_grad)[0]]
    first = (lax.axis_index("ens") == 0).astype(jnp.float32)
    misc = jnp.zeros((8, width), jnp.float32)
    misc = misc.at[0].set(partial_grads[0][0])
    misc = misc.at[1].set(partial_grads[4][0])
    misc = misc.at[2].set(head_grads[0] * first)
    misc = misc.at[3].set(head_grads[1] * first)
    table_size = partial_grads[3].size
    misc = misc.at[4, :table_size].set(partial_grads[3].reshape(-1))
    pieces = [partial_grads[1], partial_grads[2], partial_grads[5], partial_grads[6], partial_grads[7], misc]
    flat = [piece.reshape(-1, width) for piece in pieces]
    offsets = [0]
    for piece in flat:
        offsets.append(offsets[-1] + piece.shape[0])
    steps = halving_steps((("dp", lax.axis_size("dp")), ("ens", lax.axis_size("ens"))))
    first, rest = steps[0], steps[1:]
    near = [("dp", 2), ("ens", 1), ("ens", 4)]
    far = [("ens", 16), ("ens", 2), ("ens", 8)]
    assert sorted(near + far) == sorted(rest)
    count = len(near)
    orders = [near[c:] + near[:c] for c in range(count)]
    quantum = 2 * count << len(near)
    padded = -(-offsets[-1] // quantum) * quantum
    flat.append(jnp.zeros((padded - offsets[-1], width), jnp.float32))
    reduced = ring_all_reduce(jnp.concatenate(flat, axis=0), first, orders, far)
    grad_qkv, grad_out, grad_up, grad_down, grad_phi, misc = [
        reduced[offsets[k] : offsets[k + 1]].reshape(pieces[k].shape) for k in range(len(pieces))
    ]
    return (
        neg_loglik[None, :],
        misc[0][None, :],
        grad_qkv,
        grad_out,
        misc[4, :table_size].reshape(partial_grads[3].shape),
        misc[1][None, :],
        grad_up,
        grad_down,
        grad_phi,
        misc[2],
        misc[3],
    )


def solution(mesh):
    in_specs = (
        P("dp", "ens", None, None),
        P("dp", "ens"),
        P("dp", "ens"),
        P("dp", "ens", None, None),
        P("dp", None),
        P(),
        P(),
        P(),
        P(),
        P(),
        P(),
        P(),
        P(),
        P(),
        P(),
    )
    out_specs = (P("dp", None), P(), P(), P(), P(), P(), P(), P(), P(), P(), P())
    return jax.shard_map(shards, mesh=mesh, in_specs=in_specs, out_specs=out_specs, check_vma=False)
```

```python
import math

import jax
import jax.numpy as jnp
from jax import lax
from jax.sharding import PartitionSpec as P


def normalize(stream, gain_vec):
    average = jnp.mean(stream, axis=-1, keepdims=True)
    centred = stream - average
    variance = jnp.mean(centred * centred, axis=-1, keepdims=True)
    return centred * lax.rsqrt(variance + 1e-05) * gain_vec


def lookup_value(table, pair_bins):
    heads = table.shape[1]
    shape = (pair_bins.shape[0], heads) + pair_bins.shape[1:]
    levels = pair_bins[:, None, :, :]
    values = [table[level][None, :, None, None] for level in range(table.shape[0])]
    bit = 0
    while len(values) > 1:
        if len(values) % 2:
            values.append(values[-1])
        chosen = (levels >> bit) % 2 == 1
        values = [jnp.where(chosen, values[k + 1], values[k]) for k in range(0, len(values), 2)]
        bit += 1
    return jnp.broadcast_to(values[0], shape)


@jax.custom_vjp
def bias_lookup(table, pair_bins):
    return lookup_value(table, pair_bins)


def bias_lookup_fwd(table, pair_bins):
    return lookup_value(table, pair_bins), (pair_bins, table)


def bias_lookup_bwd(residuals, grad):
    pair_bins, table = residuals
    levels = jnp.arange(table.shape[0], dtype=jnp.int32)
    onehot = (pair_bins[..., None] == levels).astype(jnp.float32)
    table_grad = jnp.einsum("jqkb,jhqk->bh", onehot, grad, precision=lax.Precision.HIGHEST)
    return table_grad, None


bias_lookup.defvjp(bias_lookup_fwd, bias_lookup_bwd)


def encoder(packed, jets, lengths, pair_bins):
    gain_attn, w_qkv, w_out, pair_table, gain_ffn, w_up, w_down, w_phi = packed
    count_jets, slots, width = jets.shape
    heads = pair_table.shape[2]
    head_dim = width // heads
    live_keys = jnp.arange(slots, dtype=jnp.int32)[None, :] < lengths[:, None]
    stream = jets
    pair_bias = bias_lookup(pair_table[0], pair_bins)
    normed = (
        normalize(stream.astype(jnp.float32), gain_attn[0])
        .astype(jnp.bfloat16)
        .reshape(count_jets * slots, width)
    )
    projected = jnp.dot(normed, w_qkv[0], preferred_element_type=jnp.float32).astype(jnp.bfloat16)
    projected = projected.reshape(count_jets, slots, 3, heads, head_dim)
    queries = projected[:, :, 0]
    key_rows = projected[:, :, 1]
    value_rows = projected[:, :, 2]
    scores = (
        jnp.einsum("jqhe,jkhe->jhqk", queries, key_rows, preferred_element_type=jnp.float32)
        / math.sqrt(head_dim)
        + pair_bias
    )
    scores = jnp.where(live_keys[:, None, None, :], scores, -1e30)
    attend = jax.nn.softmax(scores, axis=-1).astype(jnp.bfloat16)
    context = jnp.einsum(
        "jhqk,jkhe->jqhe", attend, value_rows, preferred_element_type=jnp.float32
    ).astype(jnp.bfloat16)
    context = context.reshape(count_jets * slots, width)
    middle = stream.astype(jnp.float32).reshape(count_jets * slots, width) + jnp.dot(
        context, w_out[0], preferred_element_type=jnp.float32
    )
    normed = normalize(middle, gain_ffn[0]).astype(jnp.bfloat16)
    hidden = jax.nn.gelu(jnp.dot(normed, w_up[0], preferred_element_type=jnp.float32)).astype(
        jnp.bfloat16
    )
    stream = (middle + jnp.dot(hidden, w_down[0], preferred_element_type=jnp.float32)).astype(
        jnp.bfloat16
    )
    stream = stream.reshape(count_jets, slots, width)
    pooled = jnp.sum(jnp.where(live_keys[..., None], stream.astype(jnp.float32), 0.0), axis=1)
    pooled = (pooled / lengths[:, None].astype(jnp.float32)).astype(jnp.bfloat16)
    return jax.nn.gelu(jnp.dot(pooled, w_phi, preferred_element_type=jnp.float32))


def flow_head(head_weights, summed, number, masses):
    w_mean, w_scale = head_weights
    average = summed / number[..., None]
    centre = jnp.sum(average * w_mean, axis=-1)
    log_width = jnp.sum(average * w_scale, axis=-1)
    return 0.5 * jnp.square((masses - centre) * jnp.exp(-log_width)) + log_width


def butterfly_sum(value, axis, size):
    step = 1
    while step < size:
        pairs = [(index, index ^ step) for index in range(size)]
        value = value + lax.ppermute(value, axis, pairs)
        step *= 2
    return value


def halving_steps(mesh_sizes):
    steps = []
    for axis, size in mesh_sizes:
        step = 1
        while step < size:
            steps.append((axis, step))
            step *= 2
    return steps


def halve_sum(buffer, axis, step, dim=0):
    rows = buffer.shape[dim] // 2
    side = (lax.axis_index(axis) // step) % 2
    keep = lax.dynamic_slice_in_dim(buffer, side * rows, rows, dim)
    send = lax.dynamic_slice_in_dim(buffer, (1 - side) * rows, rows, dim)
    size = lax.axis_size(axis)
    pairs = [(index, index ^ step) for index in range(size)]
    return keep + lax.ppermute(send, axis, pairs)


def double_gather(buffer, axis, step, dim=0):
    rows = buffer.shape[dim]
    side = (lax.axis_index(axis) // step) % 2
    size = lax.axis_size(axis)
    pairs = [(index, index ^ step) for index in range(size)]
    other = lax.ppermute(buffer, axis, pairs)
    shape = list(buffer.shape)
    shape[dim] = 2 * rows
    whole = jnp.zeros(shape, buffer.dtype)
    whole = lax.dynamic_update_slice_in_dim(whole, buffer, side * rows, dim)
    return lax.dynamic_update_slice_in_dim(whole, other, (1 - side) * rows, dim)


def ring_all_reduce(buffer, first, orders, common):
    buffer = halve_sum(buffer, *first)
    colors = jnp.split(buffer, len(orders), axis=0)
    for step_index in range(len(orders[0])):
        colors = [halve_sum(part, *order[step_index]) for part, order in zip(colors, orders)]
    stacked = jnp.stack(colors)
    for axis, step in common:
        size = lax.axis_size(axis)
        pairs = [(index, index ^ step) for index in range(size)]
        stacked = stacked + lax.ppermute(stacked, axis, pairs)
    colors = [stacked[k] for k in range(len(orders))]
    for step_index in reversed(range(len(orders[0]))):
        colors = [double_gather(part, *order[step_index]) for part, order in zip(colors, orders)]
    return double_gather(jnp.concatenate(colors, axis=0), *first)


def shards(
    embed,
    counts,
    member,
    bins,
    masses,
    gain_attn,
    w_qkv,
    w_out,
    pair_table,
    gain_ffn,
    w_up,
    w_down,
    w_phi,
    w_mean,
    w_scale,
):
    packed = (gain_attn, w_qkv, w_out, pair_table, gain_ffn, w_up, w_down, w_phi)
    jets = embed[0]
    lengths = counts[0]
    pair_bins = bins[0]
    group_masses = masses[0]
    groups_total = group_masses.shape[0]
    width = w_phi.shape[1]

    def local_part(params_in):
        return encoder(params_in, jets, lengths, pair_bins)

    phi, back_trunk = jax.vjp(local_part, packed)
    group_onehot = (member[0][:, None] == jnp.arange(groups_total, dtype=jnp.int32)).astype(
        jnp.float32
    )
    partial_sum = jnp.dot(group_onehot.T, phi, precision=lax.Precision.HIGHEST)
    tally = jnp.sum(group_onehot, axis=0)
    stacked = jnp.concatenate(
        [partial_sum, jnp.zeros((1, width), jnp.float32).at[0, :groups_total].set(tally)], axis=0
    )
    stacked = butterfly_sum(stacked, "ens", lax.axis_size("ens"))
    summed = stacked[:groups_total]
    number = stacked[groups_total, :groups_total]

    def head_part(head_weights, summed_in):
        return flow_head(head_weights, summed_in, number, group_masses)

    neg_loglik, back_head = jax.vjp(head_part, (w_mean, w_scale), summed)
    scale_total = 1.0 / (lax.axis_size("dp") * groups_total)
    head_grads, summed_grad = back_head(jnp.full(neg_loglik.shape, scale_total, jnp.float32))
    phi_grad = jnp.dot(group_onehot, summed_grad, precision=lax.Precision.HIGHEST)
    partial_grads = [piece.astype(jnp.float32) for piece in back_trunk(phi_grad)[0]]
    first = (lax.axis_index("ens") == 0).astype(jnp.float32)
    misc = jnp.zeros((8, width), jnp.float32)
    misc = misc.at[0].set(partial_grads[0][0])
    misc = misc.at[1].set(partial_grads[4][0])
    misc = misc.at[2].set(head_grads[0] * first)
    misc = misc.at[3].set(head_grads[1] * first)
    table_size = partial_grads[3].size
    misc = misc.at[4, :table_size].set(partial_grads[3].reshape(-1))
    pieces = [partial_grads[1], partial_grads[2], partial_grads[5], partial_grads[6], partial_grads[7], misc]
    flat = [
        block
        for piece in pieces
        for block in jnp.split(piece.reshape(-1, piece.shape[-1]), piece.shape[-1] // width, axis=1)
    ]
    offsets = [0]
    for piece in flat:
        offsets.append(offsets[-1] + piece.shape[0])
    steps = halving_steps((("dp", lax.axis_size("dp")), ("ens", lax.axis_size("ens"))))
    first, rest = steps[0], steps[1:]
    near = [("dp", 2), ("ens", 1), ("ens", 4)]
    far = [("ens", 16), ("ens", 2), ("ens", 8)]
    assert sorted(near + far) == sorted(rest)
    count = len(near)
    orders = [near[c:] + near[:c] for c in range(count)]
    quantum = 2 * count << len(near)
    padded = -(-offsets[-1] // quantum) * quantum
    flat.append(jnp.zeros((padded - offsets[-1], width), jnp.float32))
    reduced = ring_all_reduce(jnp.concatenate(flat, axis=0), first, orders, far)
    blocks = [reduced[offsets[k] : offsets[k + 1]] for k in range(len(flat) - 1)]
    unpacked = []
    for piece in pieces:
        parts = piece.shape[-1] // width
        unpacked.append(jnp.concatenate(blocks[:parts], axis=1).reshape(piece.shape))
        blocks = blocks[parts:]
    grad_qkv, grad_out, grad_up, grad_down, grad_phi, misc = unpacked
    return (
        neg_loglik[None, :],
        misc[0][None, :],
        grad_qkv,
        grad_out,
        misc[4, :table_size].reshape(partial_grads[3].shape),
        misc[1][None, :],
        grad_up,
        grad_down,
        grad_phi,
        misc[2],
        misc[3],
    )


def solution(mesh):
    in_specs = (
        P("dp", "ens", None, None),
        P("dp", "ens"),
        P("dp", "ens"),
        P("dp", "ens", None, None),
        P("dp", None),
        P(),
        P(),
        P(),
        P(),
        P(),
        P(),
        P(),
        P(),
        P(),
        P(),
    )
    out_specs = (P("dp", None), P(), P(), P(), P(), P(), P(), P(), P(), P(), P())
    return jax.shard_map(shards, mesh=mesh, in_specs=in_specs, out_specs=out_specs, check_vma=False)
```
